32 devices in a mesh: dp: 16 (over z, y, core), ctx: 2 (over x).
Axes of the slice: x: 2, y: 2, z: 4, core: 2. Of those that a mesh axis runs over, the one named last changes fastest.
Arguments:
- tokens: bfloat16 [16, 2, 384, 8192], P('dp', 'ctx'), may hold values from -6 to 6
- lengths: int32 [16, 2], P('dp'), may hold values from 96 to 384, as said below
- norm_gain: float32 [8192], replicated, may hold values from 0.5 to 1.5
- w_in: bfloat16 [8192, 1536], P('dp'), may hold values from -0.0625 to 0.0625
- short_filter: float32 [3, 1536], replicated, may hold values from -3.5 to 3.5
- decay_rate: float32 [16, 512], replicated, may hold values from 5e-05 to 0.03
- residue: float32 [16, 512], replicated, may hold values from -0.12 to 0.12
- skip_gain: float32 [512], replicated, may hold values from -6 to 6
- w_out: bfloat16 [512, 8192], P(None, 'dp'), may hold values from -0.25 to 0.25
- steer_table: float32 [50, 2, 8192], replicated, may hold values from -3 to 3
- steer_layer: int32 [16], P('dp'), may hold values from 0 to 49
- steer_slab: int32 [16], P('dp'), may hold values from 0 to 7
Outputs:
- result: bfloat16 [16, 2, 384, 8192], P('dp', 'ctx')
The draws below stay inside these ranges and needn't reach their ends.
Inputs may be any that keep to these rules, and one draw needn't show every extreme that they name: `lengths`: each group holds 96 to 384 live tokens; in every sequence one group holds exactly 384.
All inputs are finite; a program needn't handle non-finite values.
Results may differ from the reference program's by a relative error of at most 0.004.
The reference program's roundings to bfloat16 on the way (of `normed`, `proj` and `gated`) count: a program that leaves them out, or rounds other values in their place, can miss the bound.
Values may be sent and summed in bfloat16 or wider, within the bound.
No kernel may reach another device: no remote copies, remote signals or barrier semaphores. Data moves between devices by JAX's collectives and lax.ppermute only.
A program may use at most 192 MiB of HBM per device.

```python
import math
import jax
import jax.numpy as jnp
from jax import lax

D = 8192
SLAB = 512
MODES = 16
STEER_W = 1024
LAYERS = 50
CAP = 384
SEQS = 16
GROUPS = 2


def draw_lengths(key, part):
    first_key, second_key = jax.random.split(jax.random.fold_in(key, 17))
    base = jax.random.randint(first_key, (SEQS, GROUPS), CAP // 4, CAP + 1)
    picked = jax.random.randint(second_key, (SEQS, 1), 0, GROUPS)
    column = jnp.arange(GROUPS)[None, :]
    return jnp.where(column == picked, CAP, base).astype(jnp.int32)


def with_ends(result, stream_key, low, top_value):
    spot = [jax.random.randint(jax.random.fold_in(stream_key, axis), (), 0, length) for axis, length in enumerate(result.shape)]
    widest = result.shape.index(max(result.shape))
    neighbour = spot[:widest] + [(spot[widest] + 1) % result.shape[widest]] + spot[widest + 1:]
    return result.at[tuple(spot)].set(low).at[tuple(neighbour)].set(top_value)


def level_of(own_key, dims, pieces, least, high):
    level, own = 1.0, jax.random.fold_in(own_key, 6)
    for dim, shards_of in pieces:
        heights = jnp.exp(jax.random.uniform(jax.random.fold_in(own, dim), (shards_of,), jnp.float32, least / len(pieces), high / len(pieces)))
        level = level * jnp.repeat(heights, dims[dim] // shards_of).reshape([-1 if axis == dim else 1 for axis in range(len(dims))])
    return level


def normal_values(own_key, dims, scale, reach, pieces=(), dtype=jnp.bfloat16):
    values = scale * jax.random.normal(own_key, dims, jnp.float32)
    if pieces:
        values = values * level_of(own_key, dims, pieces, -0.22, 0.18)
    return jnp.clip(values, -reach, reach).astype(dtype)


def setup_inputs(seed: int = 0) -> dict:
    streams_of = jax.random.split(jax.random.key(seed), 13)
    tokens = normal_values(streams_of[0], (SEQS, GROUPS, CAP, D), 1.0, 6.0, ((0, 16), (1, 2)))
    lengths = draw_lengths(jax.random.fold_in(streams_of[12], 71), 0)
    norm_gain = jnp.clip(1.0 + 0.1 * jax.random.normal(streams_of[2], (D,), jnp.float32), 0.5, 1.5)
    w_in = normal_values(streams_of[3], (D, 3 * SLAB), D ** -0.5, 0.0625, ((0, 16),))
    short_filter = normal_values(streams_of[4], (3, 3 * SLAB), 3 ** -0.5, 3.5, (), jnp.float32)
    decay_rate = jnp.clip(jnp.exp(jax.random.uniform(streams_of[5], (MODES, SLAB), jnp.float32, math.log(4.999999873689376e-05), math.log(0.03))), 4.999999873689376e-05, 0.03)
    residue = normal_values(streams_of[6], (MODES, SLAB), 0.02, 0.12, (), jnp.float32)
    skip_gain = normal_values(streams_of[7], (SLAB,), 1.0, 6.0, (), jnp.float32)
    w_out = normal_values(streams_of[8], (SLAB, D), SLAB ** -0.5, 0.25, ((1, 16),))
    steer_table = normal_values(streams_of[9], (LAYERS, 2, D), 0.5, 3.0, (), jnp.float32)
    steer_layer = with_ends(jax.random.randint(streams_of[10], (SEQS,), 0, LAYERS), jax.random.fold_in(streams_of[10], 1), 0, LAYERS - 1).astype(jnp.int32)
    steer_slab = with_ends(jax.random.randint(streams_of[11], (SEQS,), 0, D // STEER_W), jax.random.fold_in(streams_of[11], 1), 0, (D // STEER_W) - 1).astype(jnp.int32)
    return dict(tokens=tokens, lengths=lengths, norm_gain=norm_gain, w_in=w_in, short_filter=short_filter, decay_rate=decay_rate, residue=residue, skip_gain=skip_gain, w_out=w_out, steer_table=steer_table, steer_layer=steer_layer, steer_slab=steer_slab)


def normalize(rows_in, gain):
    values = rows_in.astype(jnp.float32)
    scale = lax.rsqrt(lax.optimization_barrier(jnp.mean(values * values, axis=1, keepdims=True)) + 1e-06)
    return (values * scale * gain[None, :]).astype(jnp.bfloat16)

def reference(tokens, lengths, norm_gain, w_in, short_filter, decay_rate, residue, skip_gain, w_out, steer_table, steer_layer, steer_slab):
    columns = jnp.arange(D) // STEER_W
    rate_step = jnp.exp(-decay_rate)

    def one_sequence(item):
        seq_tokens, seq_lens, layer_pick, slab_pick = item
        rows2 = lax.dynamic_index_in_dim(steer_table, layer_pick, 0, keepdims=False)
        shift_vec = rows2[0] - rows2[1]
        steer = jnp.where(columns == slab_pick, 2.0 * shift_vec, 0.0)
        rows_in = seq_tokens.reshape(GROUPS * CAP, D)
        normed = normalize(rows_in, norm_gain)
        proj = jnp.dot(normed, w_in, preferred_element_type=jnp.float32).astype(jnp.bfloat16)
        proj = lax.optimization_barrier(proj).astype(jnp.float32)
        alive_all = (jnp.arange(CAP)[None, :] < seq_lens[:, None]).reshape(-1)

        def advance(carry, step_item):
            state, last_row, before_row = carry
            row, alive = step_item
            feat = short_filter[0] * row + short_filter[1] * last_row + short_filter[2] * before_row
            gate = feat[:SLAB]
            drive = feat[SLAB:2 * SLAB] * feat[2 * SLAB:]
            new_state = rate_step * state + drive[None, :]
            filtered = lax.optimization_barrier(jnp.sum(residue * new_state, axis=0)) + skip_gain * drive
            state = jnp.where(alive, new_state, state)
            before_row = jnp.where(alive, last_row, before_row)
            last_row = jnp.where(alive, row, last_row)
            return ((state, last_row, before_row), gate * filtered)
        start = (jnp.zeros((MODES, SLAB), jnp.float32), jnp.zeros((3 * SLAB,), jnp.float32), jnp.zeros((3 * SLAB,), jnp.float32))
        _, gated = lax.scan(advance, start, (proj, alive_all))
        gated = gated.astype(jnp.bfloat16)
        mixed = jnp.dot(gated, w_out, preferred_element_type=jnp.float32)
        summed = rows_in.astype(jnp.float32) + mixed + steer[None, :]
        summed = jnp.where(alive_all[:, None], summed, 0.0)
        return summed.astype(jnp.bfloat16).reshape(GROUPS, CAP, D)
    return lax.map(one_sequence, (tokens, lengths, steer_layer, steer_slab))
```

```python
import jax
import jax.numpy as jnp
from jax import lax
from jax.sharding import PartitionSpec as P

STEER_W = 1024
CHUNKS = 4
BLOCK = 32


def from_behind(value, axis, steps):
    count = lax.axis_size(axis)
    first, last = (max(0, -steps), min(count, count - steps))
    return lax.ppermute(value, axis, [(source, source + steps) for source in range(first, last)])


def normalize(rows_in, gain):
    values = rows_in.astype(jnp.float32)
    scale = lax.rsqrt(jnp.mean(values * values, axis=1, keepdims=True) + 1e-06)
    return (values * scale * gain[None, :]).astype(jnp.bfloat16)


def filter_tables(decay_rate, residue, block):
    lags = jnp.arange(block)
    lags_float = lags.astype(jnp.float32)
    taps = jnp.sum(residue[None] * jnp.exp(-decay_rate[None] * lags_float[:, None, None]), axis=1)
    diff = lags[:, None] - lags[None, :]
    toeplitz = jnp.where((diff >= 0)[:, :, None], taps[jnp.clip(diff, 0, block - 1)], 0.0)
    lead = residue[None] * jnp.exp(-decay_rate[None] * (lags_float + 1.0)[:, None, None])
    close = jnp.exp(-decay_rate[None] * (block - 1 - lags_float)[:, None, None])
    return toeplitz, lead, close


def local_filter(drive, decay_rate, toeplitz, lead, close, block):
    cap, width = drive.shape
    count = cap // block
    pieces = drive.reshape(count, block, width)
    inside = jnp.sum(toeplitz[None] * pieces[:, None, :, :], axis=2)
    ends = jnp.sum(close[None] * pieces[:, :, None, :], axis=1)
    steps = jnp.arange(count)
    gap = (steps[:, None] - steps[None, :]).astype(jnp.float32)
    powers = jnp.where(
        (gap >= 0)[:, :, None, None],
        jnp.exp(-decay_rate[None, None] * (block * jnp.maximum(gap, 0.0))[:, :, None, None]),
        0.0,
    )
    states = jnp.sum(powers * ends[None], axis=1)
    before = jnp.concatenate([jnp.zeros_like(states[:1]), states[:-1]], axis=0)
    earlier = jnp.sum(lead[None] * before[:, None, :, :], axis=2)
    return (inside + earlier).reshape(cap, width), states[-1]


def per_device(
    tokens,
    lengths,
    norm_gain,
    w_in,
    short_filter,
    decay_rate,
    residue,
    skip_gain,
    w_out,
    steer_table,
    steer_layer,
    steer_slab,
):
    cap = tokens.shape[2]
    width = tokens.shape[3]
    slab = residue.shape[1]
    groups = lax.axis_size("ctx")
    rows_in = tokens.reshape(cap, width)
    normed = normalize(rows_in, norm_gain)
    position = lax.axis_index("ctx")
    group_lens = lengths.reshape(-1)
    own_len = lax.dynamic_index_in_dim(group_lens, position, 0, keepdims=False)
    live = jnp.arange(cap) < own_len
    own_tail = lax.dynamic_slice_in_dim(normed, own_len - 2, 2, 0)
    tail_normed = from_behind(own_tail, "ctx", 1)

    block = BLOCK if cap % BLOCK == 0 else cap
    toeplitz, lead, close = filter_tables(decay_rate, residue, block)

    lens_f = group_lens.astype(jnp.float32)
    cumlen = jnp.cumsum(lens_f)
    after = jnp.arange(cap).astype(jnp.float32) + 1.0
    rescale = jnp.exp(decay_rate * (cap - own_len).astype(jnp.float32))

    n = slab // CHUNKS
    mixed = None
    for j in range(CHUNKS):
        cols = slice(j * n, (j + 1) * n)
        piece = jnp.concatenate(
            [
                w_in[:, j * n : (j + 1) * n],
                w_in[:, slab + j * n : slab + (j + 1) * n],
                w_in[:, 2 * slab + j * n : 2 * slab + (j + 1) * n],
                w_out[j * n : (j + 1) * n, :].T,
            ],
            axis=1,
        )
        gathered = lax.all_gather(piece, "dp", axis=0, tiled=True)
        w_in_j = gathered[:, : 3 * n]
        w_out_t = gathered[:, 3 * n :]
        proj = jnp.dot(normed, w_in_j, preferred_element_type=jnp.float32).astype(jnp.bfloat16)
        tail = jnp.dot(tail_normed, w_in_j, preferred_element_type=jnp.float32).astype(jnp.bfloat16)
        extended = jnp.concatenate([tail, proj], axis=0).astype(jnp.float32)
        sf = jnp.concatenate(
            [
                short_filter[:, j * n : (j + 1) * n],
                short_filter[:, slab + j * n : slab + (j + 1) * n],
                short_filter[:, 2 * slab + j * n : 2 * slab + (j + 1) * n],
            ],
            axis=1,
        )
        feat = sf[0] * extended[2:] + sf[1] * extended[1:-1] + sf[2] * extended[:-2]
        gate = feat[:, :n]
        drive = jnp.where(live[:, None], feat[:, n : 2 * n] * feat[:, 2 * n :], 0.0)
        rate = decay_rate[:, cols]
        local, final_state = local_filter(
            drive, rate, toeplitz[:, :, cols], lead[:, :, cols], close[:, :, cols], block
        )
        ending = final_state * rescale[:, cols]
        incoming = jnp.zeros_like(ending)
        for k in range(1, groups):
            got = from_behind(ending, "ctx", k)
            source = position - k
            between = (
                lax.dynamic_index_in_dim(cumlen, jnp.maximum(position - 1, 0), 0, keepdims=False)
                - lax.dynamic_index_in_dim(cumlen, jnp.maximum(source, 0), 0, keepdims=False)
            )
            weight = jnp.where(source >= 0, jnp.exp(-rate * between), 0.0)
            incoming = incoming + weight * got
        reach = residue[None, :, cols] * jnp.exp(-rate[None] * after[:, None, None])
        crossing = jnp.sum(reach * incoming[None], axis=1)
        filtered = local + crossing + skip_gain[None, cols] * drive
        gated = jnp.where(live[:, None], gate * filtered, 0.0).astype(jnp.bfloat16)
        part = lax.dot_general(
            gated, w_out_t, (((1,), (1,)), ((), ())), preferred_element_type=jnp.float32
        )
        mixed = part if mixed is None else mixed + part
    rows2 = lax.dynamic_index_in_dim(steer_table, steer_layer[0], 0, keepdims=False)
    shift_vec = rows2[0] - rows2[1]
    columns = jnp.arange(width) // STEER_W
    steer = jnp.where(columns == steer_slab[0], 2.0 * shift_vec, 0.0)
    summed = rows_in.astype(jnp.float32) + mixed + steer[None, :]
    summed = jnp.where(live[:, None], summed, 0.0)
    return summed.astype(jnp.bfloat16).reshape(tokens.shape)


def solution(mesh):
    placed = (
        P("dp", "ctx", None, None),
        P("dp", None),
        P(),
        P("dp", None),
        P(),
        P(),
        P(),
        P(),
        P(None, "dp"),
        P(),
        P("dp"),
        P("dp"),
    )
    return jax.shard_map(
        per_device,
        mesh=mesh,
        in_specs=placed,
        out_specs=P("dp", "ctx", None, None),
        check_vma=False,
    )
```

```python
import jax
import jax.numpy as jnp
from jax import lax
from jax.sharding import PartitionSpec as P

STEER_W = 1024
BLOCK = 32


def from_behind(value, axis, steps):
    count = lax.axis_size(axis)
    first, last = (max(0, -steps), min(count, count - steps))
    return lax.ppermute(value, axis, [(source, source + steps) for source in range(first, last)])


def normalize(rows_in, gain):
    values = rows_in.astype(jnp.float32)
    scale = lax.rsqrt(jnp.mean(values * values, axis=1, keepdims=True) + 1e-06)
    return (values * scale * gain[None, :]).astype(jnp.bfloat16)


def filter_tables(decay_rate, residue, block):
    lags = jnp.arange(block)
    lags_float = lags.astype(jnp.float32)
    taps = jnp.sum(residue[None] * jnp.exp(-decay_rate[None] * lags_float[:, None, None]), axis=1)
    diff = lags[:, None] - lags[None, :]
    toeplitz = jnp.where((diff >= 0)[:, :, None], taps[jnp.clip(diff, 0, block - 1)], 0.0)
    lead = residue[None] * jnp.exp(-decay_rate[None] * (lags_float + 1.0)[:, None, None])
    close = jnp.exp(-decay_rate[None] * (block - 1 - lags_float)[:, None, None])
    return toeplitz, lead, close


def local_filter(drive, decay_rate, toeplitz, lead, close, block):
    cap, width = drive.shape
    count = cap // block
    pieces = drive.reshape(count, block, width)
    inside = jnp.sum(toeplitz[None] * pieces[:, None, :, :], axis=2)
    ends = jnp.sum(close[None] * pieces[:, :, None, :], axis=1)
    steps = jnp.arange(count)
    gap = (steps[:, None] - steps[None, :]).astype(jnp.float32)
    powers = jnp.where(
        (gap >= 0)[:, :, None, None],
        jnp.exp(-decay_rate[None, None] * (block * jnp.maximum(gap, 0.0))[:, :, None, None]),
        0.0,
    )
    states = jnp.sum(powers * ends[None], axis=1)
    before = jnp.concatenate([jnp.zeros_like(states[:1]), states[:-1]], axis=0)
    earlier = jnp.sum(lead[None] * before[:, None, :, :], axis=2)
    return (inside + earlier).reshape(cap, width), states[-1]


def per_device(
    tokens,
    lengths,
    norm_gain,
    w_in,
    short_filter,
    decay_rate,
    residue,
    skip_gain,
    w_out,
    steer_table,
    steer_layer,
    steer_slab,
):
    cap = tokens.shape[2]
    width = tokens.shape[3]
    slab = residue.shape[1]
    groups = lax.axis_size("ctx")
    rows_in = tokens.reshape(cap, width)
    normed = normalize(rows_in, norm_gain)
    position = lax.axis_index("ctx")
    group_lens = lengths.reshape(-1)
    own_len = lax.dynamic_index_in_dim(group_lens, position, 0, keepdims=False)
    live = jnp.arange(cap) < own_len
    own_tail = lax.dynamic_slice_in_dim(normed, own_len - 2, 2, 0)
    tail_normed = from_behind(own_tail, "ctx", 1)

    block = BLOCK if cap % BLOCK == 0 else cap
    toeplitz, lead, close = filter_tables(decay_rate, residue, block)

    lens_f = group_lens.astype(jnp.float32)
    cumlen = jnp.cumsum(lens_f)
    after = jnp.arange(cap).astype(jnp.float32) + 1.0
    rescale = jnp.exp(decay_rate * (cap - own_len).astype(jnp.float32))

    piece = jnp.concatenate([w_in, w_out.T], axis=1)
    gathered = lax.all_gather(piece, "dp", axis=0, tiled=True)
    w_in_all = gathered[:, : 3 * slab]
    w_out_t = gathered[:, 3 * slab :]
    proj = jnp.dot(normed, w_in_all, preferred_element_type=jnp.float32).astype(jnp.bfloat16)
    tail = jnp.dot(tail_normed, w_in_all, preferred_element_type=jnp.float32).astype(jnp.bfloat16)
    extended = jnp.concatenate([tail, proj], axis=0).astype(jnp.float32)
    feat = (
        short_filter[0] * extended[2:]
        + short_filter[1] * extended[1:-1]
        + short_filter[2] * extended[:-2]
    )
    gate = feat[:, :slab]
    drive = jnp.where(live[:, None], feat[:, slab : 2 * slab] * feat[:, 2 * slab :], 0.0)
    local, final_state = local_filter(drive, decay_rate, toeplitz, lead, close, block)
    ending = final_state * rescale
    incoming = jnp.zeros_like(ending)
    for k in range(1, groups):
        got = from_behind(ending, "ctx", k)
        source = position - k
        between = lax.dynamic_index_in_dim(
            cumlen, jnp.maximum(position - 1, 0), 0, keepdims=False
        ) - lax.dynamic_index_in_dim(cumlen, jnp.maximum(source, 0), 0, keepdims=False)
        weight = jnp.where(source >= 0, jnp.exp(-decay_rate * between), 0.0)
        incoming = incoming + weight * got
    reach = residue[None] * jnp.exp(-decay_rate[None] * after[:, None, None])
    crossing = jnp.sum(reach * incoming[None], axis=1)
    filtered = local + crossing + skip_gain[None, :] * drive
    gated = jnp.where(live[:, None], gate * filtered, 0.0).astype(jnp.bfloat16)
    mixed = lax.dot_general(
        gated, w_out_t, (((1,), (1,)), ((), ())), preferred_element_type=jnp.float32
    )
    rows2 = lax.dynamic_index_in_dim(steer_table, steer_layer[0], 0, keepdims=False)
    shift_vec = rows2[0] - rows2[1]
    columns = jnp.arange(width) // STEER_W
    steer = jnp.where(columns == steer_slab[0], 2.0 * shift_vec, 0.0)
    summed = rows_in.astype(jnp.float32) + mixed + steer[None, :]
    summed = jnp.where(live[:, None], summed, 0.0)
    return summed.astype(jnp.bfloat16).reshape(tokens.shape)


def solution(mesh):
    placed = (
        P("dp", "ctx", None, None),
        P("dp", None),
        P(),
        P("dp", None),
        P(),
        P(),
        P(),
        P(),
        P(None, "dp"),
        P(),
        P("dp"),
        P("dp"),
    )
    return jax.shard_map(
        per_device,
        mesh=mesh,
        in_specs=placed,
        out_specs=P("dp", "ctx", None, None),
        check_vma=False,
    )
```

```python
import jax
import jax.numpy as jnp
from jax import lax
from jax.sharding import PartitionSpec as P

STEER_W = 1024
BLOCK = 32


def from_behind(value, axis, steps):
    count = lax.axis_size(axis)
    first, last = (max(0, -steps), min(count, count - steps))
    return lax.ppermute(value, axis, [(source, source + steps) for source in range(first, last)])


def normalize(rows_in, gain):
    values = rows_in.astype(jnp.float32)
    scale = lax.rsqrt(jnp.mean(values * values, axis=1, keepdims=True) + 1e-06)
    return (values * scale * gain[None, :]).astype(jnp.bfloat16)


def filter_tables(decay_rate, residue, block):
    lags = jnp.arange(block)
    lags_float = lags.astype(jnp.float32)
    taps = jnp.sum(residue[None] * jnp.exp(-decay_rate[None] * lags_float[:, None, None]), axis=1)
    diff = lags[:, None] - lags[None, :]
    toeplitz = jnp.where((diff >= 0)[:, :, None], taps[jnp.clip(diff, 0, block - 1)], 0.0)
    lead = residue[None] * jnp.exp(-decay_rate[None] * (lags_float + 1.0)[:, None, None])
    close = jnp.exp(-decay_rate[None] * (block - 1 - lags_float)[:, None, None])
    return toeplitz, lead, close


def block_states(drive, decay_rate, close, block):
    cap, width = drive.shape
    count = cap // block
    pieces = drive.reshape(count, block, width)
    ends = jnp.sum(close[None] * pieces[:, :, None, :], axis=1)
    steps = jnp.arange(count)
    gap = (steps[:, None] - steps[None, :]).astype(jnp.float32)
    powers = jnp.where(
        (gap >= 0)[:, :, None, None],
        jnp.exp(-decay_rate[None, None] * (block * jnp.maximum(gap, 0.0))[:, :, None, None]),
        0.0,
    )
    return jnp.sum(powers * ends[None], axis=1)


def block_outputs(drive, states, incoming, decay_rate, toeplitz, lead, block):
    cap, width = drive.shape
    count = cap // block
    pieces = drive.reshape(count, block, width)
    inside = jnp.sum(toeplitz[None] * pieces[:, None, :, :], axis=2)
    starts = (jnp.arange(count) * block).astype(jnp.float32)
    carried = incoming[None] * jnp.exp(-decay_rate[None] * starts[:, None, None])
    before = jnp.concatenate([jnp.zeros_like(states[:1]), states[:-1]], axis=0) + carried
    earlier = jnp.sum(lead[None] * before[:, None, :, :], axis=2)
    return (inside + earlier).reshape(cap, width)


def per_device(
    tokens,
    lengths,
    norm_gain,
    w_in,
    short_filter,
    decay_rate,
    residue,
    skip_gain,
    w_out,
    steer_table,
    steer_layer,
    steer_slab,
):
    cap = tokens.shape[2]
    width = tokens.shape[3]
    slab = residue.shape[1]
    groups = lax.axis_size("ctx")
    rows_in = tokens.reshape(cap, width)
    normed = normalize(rows_in, norm_gain)
    position = lax.axis_index("ctx")
    group_lens = lengths.reshape(-1)
    own_len = lax.dynamic_index_in_dim(group_lens, position, 0, keepdims=False)
    live = jnp.arange(cap) < own_len
    own_tail = lax.dynamic_slice_in_dim(normed, own_len - 2, 2, 0)
    tail_normed = from_behind(own_tail, "ctx", 1)

    block = BLOCK if cap % BLOCK == 0 else cap
    toeplitz, lead, close = filter_tables(decay_rate, residue, block)

    lens_f = group_lens.astype(jnp.float32)
    cumlen = jnp.cumsum(lens_f)
    rescale = jnp.exp(decay_rate * (cap - own_len).astype(jnp.float32))

    piece = jnp.concatenate([w_in, w_out.T], axis=1)
    gathered = lax.all_gather(piece, "dp", axis=0, tiled=True)
    w_in_all = gathered[:, : 3 * slab]
    w_out_t = gathered[:, 3 * slab :]
    rows_ext = jnp.concatenate([tail_normed, normed], axis=0)
    extended = jnp.dot(rows_ext, w_in_all, preferred_element_type=jnp.float32)
    extended = extended.astype(jnp.bfloat16).astype(jnp.float32)
    feat = (
        short_filter[0] * extended[2:]
        + short_filter[1] * extended[1:-1]
        + short_filter[2] * extended[:-2]
    )
    gate = feat[:, :slab]
    drive = jnp.where(live[:, None], feat[:, slab : 2 * slab] * feat[:, 2 * slab :], 0.0)
    states = block_states(drive, decay_rate, close, block)
    ending = states[-1] * rescale
    incoming = jnp.zeros_like(ending)
    for k in range(1, groups):
        got = from_behind(ending, "ctx", k)
        source = position - k
        between = lax.dynamic_index_in_dim(
            cumlen, jnp.maximum(position - 1, 0), 0, keepdims=False
        ) - lax.dynamic_index_in_dim(cumlen, jnp.maximum(source, 0), 0, keepdims=False)
        weight = jnp.where(source >= 0, jnp.exp(-decay_rate * between), 0.0)
        incoming = incoming + weight * got
    local = block_outputs(drive, states, incoming, decay_rate, toeplitz, lead, block)
    filtered = local + skip_gain[None, :] * drive
    gated = jnp.where(live[:, None], gate * filtered, 0.0).astype(jnp.bfloat16)
    mixed = lax.dot_general(
        gated, w_out_t, (((1,), (1,)), ((), ())), preferred_element_type=jnp.float32
    )
    rows2 = lax.dynamic_index_in_dim(steer_table, steer_layer[0], 0, keepdims=False)
    shift_vec = rows2[0] - rows2[1]
    columns = jnp.arange(width) // STEER_W
    steer = jnp.where(columns == steer_slab[0], 2.0 * shift_vec, 0.0)
    summed = rows_in.astype(jnp.float32) + mixed + steer[None, :]
    summed = jnp.where(live[:, None], summed, 0.0)
    return summed.astype(jnp.bfloat16).reshape(tokens.shape)


def solution(mesh):
    placed = (
        P("dp", "ctx", None, None),
        P("dp", None),
        P(),
        P("dp", None),
        P(),
        P(),
        P(),
        P(),
        P(None, "dp"),
        P(),
        P("dp"),
        P("dp"),
    )
    return jax.shard_map(
        per_device,
        mesh=mesh,
        in_specs=placed,
        out_specs=P("dp", "ctx", None, None),
        check_vma=False,
    )
```

```python
import jax
import jax.numpy as jnp
from jax import lax
from jax.sharding import PartitionSpec as P

STEER_W = 1024
BLOCK = 32


def from_behind(value, axis, steps):
    count = lax.axis_size(axis)
    first, last = (max(0, -steps), min(count, count - steps))
    return lax.ppermute(value, axis, [(source, source + steps) for source in range(first, last)])


def normalize(rows_in, gain):
    values = rows_in.astype(jnp.float32)
    scale = lax.rsqrt(jnp.mean(values * values, axis=1, keepdims=True) + 1e-06)
    return (values * scale * gain[None, :]).astype(jnp.bfloat16)


def filter_tables(decay_rate, residue, block):
    lags = jnp.arange(block)
    lags_float = lags.astype(jnp.float32)
    taps = jnp.sum(residue[None] * jnp.exp(-decay_rate[None] * lags_float[:, None, None]), axis=1)
    diff = lags[:, None] - lags[None, :]
    toeplitz = jnp.where((diff >= 0)[:, :, None], taps[jnp.clip(diff, 0, block - 1)], 0.0)
    toeplitz = jnp.transpose(toeplitz, (1, 0, 2))
    lead = residue[:, None] * jnp.exp(-decay_rate[:, None] * (lags_float + 1.0)[None, :, None])
    close = jnp.exp(-decay_rate[None] * (block - 1 - lags_float)[:, None, None])
    return toeplitz, lead, close


def block_states(drive, decay_rate, close, block):
    cap, width = drive.shape
    count = cap // block
    pieces = drive.reshape(count, block, width)
    ends = jnp.sum(close[None] * pieces[:, :, None, :], axis=1)
    steps = jnp.arange(count)
    gap = (steps[:, None] - steps[None, :]).astype(jnp.float32)
    powers = jnp.where(
        (gap >= 0)[:, :, None, None],
        jnp.exp(-decay_rate[None, None] * (block * jnp.maximum(gap, 0.0))[:, :, None, None]),
        0.0,
    )
    return jnp.sum(powers * ends[None], axis=1)


def block_outputs(drive, states, incoming, decay_rate, toeplitz, lead, block):
    cap, width = drive.shape
    count = cap // block
    pieces = drive.reshape(count, block, width)
    inside = jnp.sum(toeplitz[None] * pieces[:, :, None, :], axis=1)
    starts = (jnp.arange(count) * block).astype(jnp.float32)
    carried = incoming[None] * jnp.exp(-decay_rate[None] * starts[:, None, None])
    before = jnp.concatenate([jnp.zeros_like(states[:1]), states[:-1]], axis=0) + carried
    earlier = jnp.sum(lead[None] * before[:, :, None, :], axis=1)
    return (inside + earlier).reshape(cap, width)


def per_device(
    tokens,
    lengths,
    norm_gain,
    w_in,
    short_filter,
    decay_rate,
    residue,
    skip_gain,
    w_out,
    steer_table,
    steer_layer,
    steer_slab,
):
    cap = tokens.shape[2]
    width = tokens.shape[3]
    slab = residue.shape[1]
    groups = lax.axis_size("ctx")
    rows_in = tokens.reshape(cap, width)
    normed = normalize(rows_in, norm_gain)
    position = lax.axis_index("ctx")
    group_lens = lengths.reshape(-1)
    own_len = lax.dynamic_index_in_dim(group_lens, position, 0, keepdims=False)
    live = jnp.arange(cap) < own_len
    own_tail = lax.dynamic_slice_in_dim(normed, own_len - 2, 2, 0)
    tail_normed = from_behind(own_tail, "ctx", 1)

    block = BLOCK if cap % BLOCK == 0 else cap
    toeplitz, lead, close = filter_tables(decay_rate, residue, block)

    lens_f = group_lens.astype(jnp.float32)
    cumlen = jnp.cumsum(lens_f)
    rescale = jnp.exp(decay_rate * (cap - own_len).astype(jnp.float32))

    piece = jnp.concatenate([w_in, w_out.T], axis=1)
    gathered = lax.all_gather(piece, "dp", axis=0, tiled=True)
    w_in_all = gathered[:, : 3 * slab]
    w_out_t = gathered[:, 3 * slab :]
    rows_ext = jnp.concatenate([tail_normed, normed], axis=0)
    extended = jnp.dot(rows_ext, w_in_all, preferred_element_type=jnp.float32)
    extended = lax.reduce_precision(extended, exponent_bits=8, mantissa_bits=7)
    feat = (
        short_filter[0] * extended[2:]
        + short_filter[1] * extended[1:-1]
        + short_filter[2] * extended[:-2]
    )
    gate = feat[:, :slab]
    drive = jnp.where(live[:, None], feat[:, slab : 2 * slab] * feat[:, 2 * slab :], 0.0)
    states = block_states(drive, decay_rate, close, block)
    ending = states[-1] * rescale
    incoming = jnp.zeros_like(ending)
    for k in range(1, groups):
        got = from_behind(ending, "ctx", k)
        source = position - k
        between = lax.dynamic_index_in_dim(
            cumlen, jnp.maximum(position - 1, 0), 0, keepdims=False
        ) - lax.dynamic_index_in_dim(cumlen, jnp.maximum(source, 0), 0, keepdims=False)
        weight = jnp.where(source >= 0, jnp.exp(-decay_rate * between), 0.0)
        incoming = incoming + weight * got
    local = block_outputs(drive, states, incoming, decay_rate, toeplitz, lead, block)
    filtered = local + skip_gain[None, :] * drive
    gated = jnp.where(live[:, None], gate * filtered, 0.0).astype(jnp.bfloat16)
    mixed = lax.dot_general(
        gated, w_out_t, (((1,), (1,)), ((), ())), preferred_element_type=jnp.float32
    )
    rows2 = lax.dynamic_index_in_dim(steer_table, steer_layer[0], 0, keepdims=False)
    shift_vec = rows2[0] - rows2[1]
    columns = jnp.arange(width) // STEER_W
    steer = jnp.where(columns == steer_slab[0], 2.0 * shift_vec, 0.0)
    summed = rows_in.astype(jnp.float32) + mixed + steer[None, :]
    summed = jnp.where(live[:, None], summed, 0.0)
    return summed.astype(jnp.bfloat16).reshape(tokens.shape)


def solution(mesh):
    placed = (
        P("dp", "ctx", None, None),
        P("dp", None),
        P(),
        P("dp", None),
        P(),
        P(),
        P(),
        P(),
        P(None, "dp"),
        P(),
        P("dp"),
        P("dp"),
    )
    return jax.shard_map(
        per_device,
        mesh=mesh,
        in_specs=placed,
        out_specs=P("dp", "ctx", None, None),
        check_vma=False,
    )
```

```python
import jax
import jax.numpy as jnp
from jax import lax
from jax.sharding import PartitionSpec as P

STEER_W = 1024
BLOCK = 32


def from_behind(value, axis, steps):
    count = lax.axis_size(axis)
    first, last = (max(0, -steps), min(count, count - steps))
    return lax.ppermute(value, axis, [(source, source + steps) for source in range(first, last)])


def normalize(rows_in, gain):
    values = rows_in.astype(jnp.float32)
    scale = lax.rsqrt(jnp.mean(values * values, axis=1, keepdims=True) + 1e-06)
    return (values * scale * gain[None, :]).astype(jnp.bfloat16)


def filter_tables(decay_rate, residue, block):
    lags = jnp.arange(block)
    lags_float = lags.astype(jnp.float32)
    taps = jnp.sum(residue[None] * jnp.exp(-decay_rate[None] * lags_float[:, None, None]), axis=1)
    diff = lags[:, None] - lags[None, :]
    toeplitz = jnp.where((diff >= 0)[:, :, None], taps[jnp.clip(diff, 0, block - 1)], 0.0)
    toeplitz = jnp.transpose(toeplitz, (1, 0, 2))
    lead = residue[:, None] * jnp.exp(-decay_rate[:, None] * (lags_float + 1.0)[None, :, None])
    close = jnp.exp(-decay_rate[None] * (block - 1 - lags_float)[:, None, None])
    return toeplitz, lead, close


def block_ends(drive, close, block):
    cap, width = drive.shape
    pieces = drive.reshape(cap // block, block, width)
    return jnp.sum(close[None] * pieces[:, :, None, :], axis=1)


def block_powers(decay_rate, count, block):
    steps = jnp.arange(count)
    gap = (steps[:, None] - steps[None, :]).astype(jnp.float32)
    return jnp.where(
        (gap >= 0)[:, :, None, None],
        jnp.exp(-decay_rate[None, None] * (block * jnp.maximum(gap, 0.0))[:, :, None, None]),
        0.0,
    )


def block_outputs(drive, states, incoming, decay_rate, toeplitz, lead, block):
    cap, width = drive.shape
    count = cap // block
    pieces = drive.reshape(count, block, width)
    inside = jnp.sum(toeplitz[None] * pieces[:, :, None, :], axis=1)
    starts = (jnp.arange(count) * block).astype(jnp.float32)
    carried = incoming[None] * jnp.exp(-decay_rate[None] * starts[:, None, None])
    before = jnp.concatenate([jnp.zeros_like(states[:1]), states[:-1]], axis=0) + carried
    earlier = jnp.sum(lead[None] * before[:, :, None, :], axis=1)
    return (inside + earlier).reshape(cap, width)


def per_device(
    tokens,
    lengths,
    norm_gain,
    w_in,
    short_filter,
    decay_rate,
    residue,
    skip_gain,
    w_out,
    steer_table,
    steer_layer,
    steer_slab,
):
    cap = tokens.shape[2]
    width = tokens.shape[3]
    slab = residue.shape[1]
    groups = lax.axis_size("ctx")
    rows_in = tokens.reshape(cap, width)
    normed = normalize(rows_in, norm_gain)
    position = lax.axis_index("ctx")
    group_lens = lengths.reshape(-1)
    own_len = lax.dynamic_index_in_dim(group_lens, position, 0, keepdims=False)
    live = jnp.arange(cap) < own_len
    own_tail = lax.dynamic_slice_in_dim(normed, own_len - 2, 2, 0)
    tail_normed = from_behind(own_tail, "ctx", 1)

    block = BLOCK if cap % BLOCK == 0 else cap
    toeplitz, lead, close = filter_tables(decay_rate, residue, block)
    powers = block_powers(decay_rate, cap // block, block)

    lens_f = group_lens.astype(jnp.float32)
    cumlen = jnp.cumsum(lens_f)
    rescale = jnp.exp(decay_rate * (cap - own_len).astype(jnp.float32))

    piece = jnp.concatenate([w_in, w_out.T], axis=1)
    gathered = lax.all_gather(piece, "dp", axis=0, tiled=True)
    w_in_all = gathered[:, : 3 * slab]
    w_out_t = gathered[:, 3 * slab :]
    rows_ext = jnp.concatenate([tail_normed, normed], axis=0)
    proj = jnp.dot(rows_ext, w_in_all, preferred_element_type=jnp.float32).astype(jnp.bfloat16)
    extended = lax.optimization_barrier(proj).astype(jnp.float32)
    feat = (
        short_filter[0] * extended[2:]
        + short_filter[1] * extended[1:-1]
        + short_filter[2] * extended[:-2]
    )
    gate = feat[:, :slab]
    drive = jnp.where(live[:, None], feat[:, slab : 2 * slab] * feat[:, 2 * slab :], 0.0)
    ends = block_ends(drive, close, block)
    ending = jnp.sum(powers[-1] * ends, axis=0) * rescale
    incoming = jnp.zeros_like(ending)
    for k in range(1, groups):
        got = from_behind(ending, "ctx", k)
        source = position - k
        between = lax.dynamic_index_in_dim(
            cumlen, jnp.maximum(position - 1, 0), 0, keepdims=False
        ) - lax.dynamic_index_in_dim(cumlen, jnp.maximum(source, 0), 0, keepdims=False)
        weight = jnp.where(source >= 0, jnp.exp(-decay_rate * between), 0.0)
        incoming = incoming + weight * got
    states = jnp.sum(powers * ends[None], axis=1)
    local = block_outputs(drive, states, incoming, decay_rate, toeplitz, lead, block)
    filtered = local + skip_gain[None, :] * drive
    gated = jnp.where(live[:, None], gate * filtered, 0.0).astype(jnp.bfloat16)
    mixed = lax.dot_general(
        gated, w_out_t, (((1,), (1,)), ((), ())), preferred_element_type=jnp.float32
    )
    rows2 = lax.dynamic_index_in_dim(steer_table, steer_layer[0], 0, keepdims=False)
    shift_vec = rows2[0] - rows2[1]
    columns = jnp.arange(width) // STEER_W
    steer = jnp.where(columns == steer_slab[0], 2.0 * shift_vec, 0.0)
    summed = rows_in.astype(jnp.float32) + mixed + steer[None, :]
    summed = jnp.where(live[:, None], summed, 0.0)
    return summed.astype(jnp.bfloat16).reshape(tokens.shape)


def solution(mesh):
    placed = (
        P("dp", "ctx", None, None),
        P("dp", None),
        P(),
        P("dp", None),
        P(),
        P(),
        P(),
        P(),
        P(None, "dp"),
        P(),
        P("dp"),
        P("dp"),
    )
    return jax.shard_map(
        per_device,
        mesh=mesh,
        in_specs=placed,
        out_specs=P("dp", "ctx", None, None),
        check_vma=False,
    )
```

```python
import jax
import jax.numpy as jnp
from jax import lax
from jax.experimental import pallas as pl
from jax.sharding import PartitionSpec as P

STEER_W = 1024
BLOCK = 32


def from_behind(value, axis, steps):
    count = lax.axis_size(axis)
    first, last = (max(0, -steps), min(count, count - steps))
    return lax.ppermute(value, axis, [(source, source + steps) for source in range(first, last)])


def normalize(rows_in, gain):
    values = rows_in.astype(jnp.float32)
    scale = lax.rsqrt(jnp.mean(values * values, axis=1, keepdims=True) + 1e-06)
    return (values * scale * gain[None, :]).astype(jnp.bfloat16)


def filter_tables(decay_rate, residue, block):
    lags = jnp.arange(block)
    lags_float = lags.astype(jnp.float32)
    taps = jnp.sum(residue[None] * jnp.exp(-decay_rate[None] * lags_float[:, None, None]), axis=1)
    diff = lags[:, None] - lags[None, :]
    toeplitz = jnp.where((diff >= 0)[:, :, None], taps[jnp.clip(diff, 0, block - 1)], 0.0)
    toeplitz = jnp.transpose(toeplitz, (1, 0, 2))
    lead = residue[:, None] * jnp.exp(-decay_rate[:, None] * (lags_float + 1.0)[None, :, None])
    close = jnp.exp(-decay_rate[None] * (block - 1 - lags_float)[:, None, None])
    return toeplitz, lead, close


def block_states(drive, decay_rate, close, block):
    cap, width = drive.shape
    count = cap // block
    pieces = drive.reshape(count, block, width)
    ends = jnp.sum(close[None] * pieces[:, :, None, :], axis=1)
    steps = jnp.arange(count)
    gap = (steps[:, None] - steps[None, :]).astype(jnp.float32)
    powers = jnp.where(
        (gap >= 0)[:, :, None, None],
        jnp.exp(-decay_rate[None, None] * (block * jnp.maximum(gap, 0.0))[:, :, None, None]),
        0.0,
    )
    return jnp.sum(powers * ends[None], axis=1)


def block_outputs(drive, states, incoming, decay_rate, toeplitz, lead, block):
    cap, width = drive.shape
    count = cap // block
    pieces = drive.reshape(count, block, width)
    inside = jnp.sum(toeplitz[None] * pieces[:, :, None, :], axis=1)
    starts = (jnp.arange(count) * block).astype(jnp.float32)
    carried = incoming[None] * jnp.exp(-decay_rate[None] * starts[:, None, None])
    before = jnp.concatenate([jnp.zeros_like(states[:1]), states[:-1]], axis=0) + carried
    earlier = jnp.sum(lead[None] * before[:, :, None, :], axis=1)
    return (inside + earlier).reshape(cap, width)


def out_kernel(g_ref, w_ref, t_ref, s_ref, m_ref, o_ref):
    acc = lax.dot_general(g_ref[...], w_ref[...], (((1,), (1,)), ((), ())), preferred_element_type=jnp.float32)
    res = t_ref[...].astype(jnp.float32) + acc + s_ref[...]
    o_ref[...] = jnp.where(m_ref[...] > 0, res, 0.0).astype(o_ref.dtype)

def project_out(gated, gathered, rows_in, steer, live, tile=1024):
    cap, slab = gated.shape
    width = rows_in.shape[1]
    column = (gathered.shape[1] - slab) // slab
    return pl.pallas_call(
        out_kernel,
        grid=(width // tile,),
        in_specs=[
            pl.BlockSpec((cap, slab), lambda j: (0, 0)),
            pl.BlockSpec((tile, slab), lambda j: (j, column)),
            pl.BlockSpec((cap, tile), lambda j: (0, j)),
            pl.BlockSpec((1, tile), lambda j: (0, j)),
            pl.BlockSpec((cap, 1), lambda j: (0, 0)),
        ],
        out_specs=pl.BlockSpec((cap, tile), lambda j: (0, j)),
        out_shape=jax.ShapeDtypeStruct((cap, width), rows_in.dtype),
        cost_estimate=pl.CostEstimate(flops=2 * cap * slab * width, transcendentals=0,
            bytes_accessed=2 * (cap * slab + width * slab + 2 * cap * width) + 4 * width),
    )(gated, gathered, rows_in, steer.reshape(1, width), live.astype(jnp.int32).reshape(cap, 1))

def per_device(
    tokens,
    lengths,
    norm_gain,
    w_in,
    short_filter,
    decay_rate,
    residue,
    skip_gain,
    w_out,
    steer_table,
    steer_layer,
    steer_slab,
):
    cap = tokens.shape[2]
    width = tokens.shape[3]
    slab = residue.shape[1]
    groups = lax.axis_size("ctx")
    rows_in = tokens.reshape(cap, width)
    normed = normalize(rows_in, norm_gain)
    position = lax.axis_index("ctx")
    group_lens = lengths.reshape(-1)
    own_len = lax.dynamic_index_in_dim(group_lens, position, 0, keepdims=False)
    live = jnp.arange(cap) < own_len
    own_tail = lax.dynamic_slice_in_dim(normed, own_len - 2, 2, 0)
    tail_normed = from_behind(own_tail, "ctx", 1)

    block = BLOCK if cap % BLOCK == 0 else cap
    toeplitz, lead, close = filter_tables(decay_rate, residue, block)

    lens_f = group_lens.astype(jnp.float32)
    cumlen = jnp.cumsum(lens_f)
    rescale = jnp.exp(decay_rate * (cap - own_len).astype(jnp.float32))

    piece = jnp.concatenate([w_in, w_out.T], axis=1)
    gathered = lax.all_gather(piece, "dp", axis=0, tiled=True)
    w_in_all = gathered[:, : 3 * slab]
    rows_ext = jnp.concatenate([tail_normed, normed], axis=0)
    extended = jnp.dot(rows_ext, w_in_all, preferred_element_type=jnp.float32)
    extended = lax.reduce_precision(extended, exponent_bits=8, mantissa_bits=7)
    feat = (
        short_filter[0] * extended[2:]
        + short_filter[1] * extended[1:-1]
        + short_filter[2] * extended[:-2]
    )
    gate = feat[:, :slab]
    drive = jnp.where(live[:, None], feat[:, slab : 2 * slab] * feat[:, 2 * slab :], 0.0)
    states = block_states(drive, decay_rate, close, block)
    ending = states[-1] * rescale
    incoming = jnp.zeros_like(ending)
    for k in range(1, groups):
        got = from_behind(ending, "ctx", k)
        source = position - k
        between = lax.dynamic_index_in_dim(
            cumlen, jnp.maximum(position - 1, 0), 0, keepdims=False
        ) - lax.dynamic_index_in_dim(cumlen, jnp.maximum(source, 0), 0, keepdims=False)
        weight = jnp.where(source >= 0, jnp.exp(-decay_rate * between), 0.0)
        incoming = incoming + weight * got
    local = block_outputs(drive, states, incoming, decay_rate, toeplitz, lead, block)
    filtered = local + skip_gain[None, :] * drive
    gated = jnp.where(live[:, None], gate * filtered, 0.0).astype(jnp.bfloat16)
    rows2 = lax.dynamic_index_in_dim(steer_table, steer_layer[0], 0, keepdims=False)
    shift_vec = rows2[0] - rows2[1]
    columns = jnp.arange(width) // STEER_W
    steer = jnp.where(columns == steer_slab[0], 2.0 * shift_vec, 0.0)
    result = project_out(gated, gathered, rows_in, steer, live)
    return result.reshape(tokens.shape)


def solution(mesh):
    placed = (
        P("dp", "ctx", None, None),
        P("dp", None),
        P(),
        P("dp", None),
        P(),
        P(),
        P(),
        P(),
        P(None, "dp"),
        P(),
        P("dp"),
        P("dp"),
    )
    return jax.shard_map(
        per_device,
        mesh=mesh,
        in_specs=placed,
        out_specs=P("dp", "ctx", None, None),
        check_vma=False,
    )
```

```python
import jax
import jax.numpy as jnp
from jax import lax
from jax.experimental import pallas as pl
from jax.sharding import PartitionSpec as P

STEER_W = 1024
BLOCK = 32


def from_behind(value, axis, steps):
    count = lax.axis_size(axis)
    first, last = (max(0, -steps), min(count, count - steps))
    return lax.ppermute(value, axis, [(source, source + steps) for source in range(first, last)])


def normalize(rows_in, gain):
    values = rows_in.astype(jnp.float32)
    scale = lax.rsqrt(jnp.mean(values * values, axis=1, keepdims=True) + 1e-06)
    return (values * scale * gain[None, :]).astype(jnp.bfloat16)


def filter_tables(decay_rate, residue, block):
    lags = jnp.arange(block)
    lags_float = lags.astype(jnp.float32)
    taps = jnp.sum(residue[None] * jnp.exp(-decay_rate[None] * lags_float[:, None, None]), axis=1)
    diff = lags[:, None] - lags[None, :]
    toeplitz = jnp.where((diff >= 0)[:, :, None], taps[jnp.clip(diff, 0, block - 1)], 0.0)
    toeplitz = jnp.transpose(toeplitz, (1, 0, 2))
    lead = residue[:, None] * jnp.exp(-decay_rate[:, None] * (lags_float + 1.0)[None, :, None])
    close = jnp.exp(-decay_rate[None] * (block - 1 - lags_float)[:, None, None])
    return toeplitz, lead, close


def block_states(drive, decay_rate, close, block):
    cap, width = drive.shape
    count = cap // block
    pieces = drive.reshape(count, block, width)
    ends = jnp.sum(close[None] * pieces[:, :, None, :], axis=1)
    steps = jnp.arange(count)
    gap = (steps[:, None] - steps[None, :]).astype(jnp.float32)
    powers = jnp.where(
        (gap >= 0)[:, :, None, None],
        jnp.exp(-decay_rate[None, None] * (block * jnp.maximum(gap, 0.0))[:, :, None, None]),
        0.0,
    )
    return jnp.sum(powers * ends[None], axis=1)


def block_outputs(drive, states, incoming, decay_rate, toeplitz, lead, block):
    cap, width = drive.shape
    count = cap // block
    pieces = drive.reshape(count, block, width)
    inside = jnp.sum(toeplitz[None] * pieces[:, :, None, :], axis=1)
    starts = (jnp.arange(count) * block).astype(jnp.float32)
    carried = incoming[None] * jnp.exp(-decay_rate[None] * starts[:, None, None])
    before = jnp.concatenate([jnp.zeros_like(states[:1]), states[:-1]], axis=0) + carried
    earlier = jnp.sum(lead[None] * before[:, :, None, :], axis=1)
    return (inside + earlier).reshape(cap, width)


def out_kernel(g_ref, w_ref, t_ref, s_ref, m_ref, o_ref):
    flipped = jnp.dot(w_ref[...], g_ref[...], preferred_element_type=jnp.float32)
    res = t_ref[...].astype(jnp.float32) + flipped.T + s_ref[...]
    o_ref[...] = jnp.where(m_ref[...] > 0, res, 0.0).astype(o_ref.dtype)


def project_out(gated, gathered, rows_in, steer, live, tile=512):
    cap, slab = gated.shape
    width = rows_in.shape[1]
    column = (gathered.shape[1] - slab) // slab
    return pl.pallas_call(
        out_kernel,
        grid=(width // tile,),
        in_specs=[
            pl.BlockSpec((slab, cap), lambda j: (0, 0)),
            pl.BlockSpec((tile, slab), lambda j: (j, column)),
            pl.BlockSpec((cap, tile), lambda j: (0, j)),
            pl.BlockSpec((1, tile), lambda j: (0, j)),
            pl.BlockSpec((cap, 1), lambda j: (0, 0)),
        ],
        out_specs=pl.BlockSpec((cap, tile), lambda j: (0, j)),
        out_shape=jax.ShapeDtypeStruct((cap, width), rows_in.dtype),
        cost_estimate=pl.CostEstimate(
            flops=2 * cap * slab * width,
            transcendentals=0,
            bytes_accessed=2 * (cap * slab + width * slab + 2 * cap * width) + 4 * width,
        ),
    )(gated.T, gathered, rows_in, steer.reshape(1, width), live.astype(jnp.int32).reshape(cap, 1))

def per_device(
    tokens,
    lengths,
    norm_gain,
    w_in,
    short_filter,
    decay_rate,
    residue,
    skip_gain,
    w_out,
    steer_table,
    steer_layer,
    steer_slab,
):
    cap = tokens.shape[2]
    width = tokens.shape[3]
    slab = residue.shape[1]
    groups = lax.axis_size("ctx")
    rows_in = tokens.reshape(cap, width)
    normed = normalize(rows_in, norm_gain)
    position = lax.axis_index("ctx")
    group_lens = lengths.reshape(-1)
    own_len = lax.dynamic_index_in_dim(group_lens, position, 0, keepdims=False)
    live = jnp.arange(cap) < own_len
    own_tail = lax.dynamic_slice_in_dim(normed, own_len - 2, 2, 0)
    tail_normed = from_behind(own_tail, "ctx", 1)

    block = BLOCK if cap % BLOCK == 0 else cap
    toeplitz, lead, close = filter_tables(decay_rate, residue, block)

    lens_f = group_lens.astype(jnp.float32)
    cumlen = jnp.cumsum(lens_f)
    rescale = jnp.exp(decay_rate * (cap - own_len).astype(jnp.float32))

    piece = jnp.concatenate([w_in, w_out.T], axis=1)
    gathered = lax.all_gather(piece, "dp", axis=0, tiled=True)
    w_in_all = gathered[:, : 3 * slab]
    rows_ext = jnp.concatenate([tail_normed, normed], axis=0)
    extended = jnp.dot(rows_ext, w_in_all, preferred_element_type=jnp.float32)
    extended = lax.reduce_precision(extended, exponent_bits=8, mantissa_bits=7)
    feat = (
        short_filter[0] * extended[2:]
        + short_filter[1] * extended[1:-1]
        + short_filter[2] * extended[:-2]
    )
    gate = feat[:, :slab]
    drive = jnp.where(live[:, None], feat[:, slab : 2 * slab] * feat[:, 2 * slab :], 0.0)
    states = block_states(drive, decay_rate, close, block)
    ending = states[-1] * rescale
    incoming = jnp.zeros_like(ending)
    for k in range(1, groups):
        got = from_behind(ending, "ctx", k)
        source = position - k
        between = lax.dynamic_index_in_dim(
            cumlen, jnp.maximum(position - 1, 0), 0, keepdims=False
        ) - lax.dynamic_index_in_dim(cumlen, jnp.maximum(source, 0), 0, keepdims=False)
        weight = jnp.where(source >= 0, jnp.exp(-decay_rate * between), 0.0)
        incoming = incoming + weight * got
    local = block_outputs(drive, states, incoming, decay_rate, toeplitz, lead, block)
    filtered = local + skip_gain[None, :] * drive
    gated = jnp.where(live[:, None], gate * filtered, 0.0).astype(jnp.bfloat16)
    rows2 = lax.dynamic_index_in_dim(steer_table, steer_layer[0], 0, keepdims=False)
    shift_vec = rows2[0] - rows2[1]
    columns = jnp.arange(width) // STEER_W
    steer = jnp.where(columns == steer_slab[0], 2.0 * shift_vec, 0.0)
    result = project_out(gated, gathered, rows_in, steer, live)
    return result.reshape(tokens.shape)


def solution(mesh):
    placed = (
        P("dp", "ctx", None, None),
        P("dp", None),
        P(),
        P("dp", None),
        P(),
        P(),
        P(),
        P(),
        P(None, "dp"),
        P(),
        P("dp"),
        P("dp"),
    )
    return jax.shard_map(
        per_device,
        mesh=mesh,
        in_specs=placed,
        out_specs=P("dp", "ctx", None, None),
        check_vma=False,
    )
```

```python
import jax
import jax.numpy as jnp
from jax import lax
from jax.experimental import pallas as pl
from jax.sharding import PartitionSpec as P

STEER_W = 1024
BLOCK = 32


def from_behind(value, axis, steps):
    count = lax.axis_size(axis)
    first, last = (max(0, -steps), min(count, count - steps))
    return lax.ppermute(value, axis, [(source, source + steps) for source in range(first, last)])


def normalize(rows_in, gain):
    values = rows_in.astype(jnp.float32)
    scale = lax.rsqrt(jnp.mean(values * values, axis=1, keepdims=True) + 1e-06)
    return (values * scale * gain[None, :]).astype(jnp.bfloat16)


def filter_tables(decay_rate, residue, block):
    lags = jnp.arange(block)
    lags_float = lags.astype(jnp.float32)
    taps = jnp.sum(residue[None] * jnp.exp(-decay_rate[None] * lags_float[:, None, None]), axis=1)
    diff = lags[:, None] - lags[None, :]
    toeplitz = jnp.where((diff >= 0)[:, :, None], taps[jnp.clip(diff, 0, block - 1)], 0.0)
    toeplitz = jnp.transpose(toeplitz, (1, 0, 2))
    lead = residue[:, None] * jnp.exp(-decay_rate[:, None] * (lags_float + 1.0)[None, :, None])
    close = jnp.exp(-decay_rate[None] * (block - 1 - lags_float)[:, None, None])
    return toeplitz, lead, close


def block_states(drive, decay_rate, close, block):
    cap, width = drive.shape
    count = cap // block
    pieces = drive.reshape(count, block, width)
    ends = jnp.sum(close[None] * pieces[:, :, None, :], axis=1)
    steps = jnp.arange(count)
    gap = (steps[:, None] - steps[None, :]).astype(jnp.float32)
    powers = jnp.where(
        (gap >= 0)[:, :, None, None],
        jnp.exp(-decay_rate[None, None] * (block * jnp.maximum(gap, 0.0))[:, :, None, None]),
        0.0,
    )
    return jnp.sum(powers * ends[None], axis=1)


def block_outputs(drive, states, incoming, decay_rate, toeplitz, lead, block):
    cap, width = drive.shape
    count = cap // block
    pieces = drive.reshape(count, block, width)
    inside = jnp.sum(toeplitz[None] * pieces[:, :, None, :], axis=1)
    starts = (jnp.arange(count) * block).astype(jnp.float32)
    carried = incoming[None] * jnp.exp(-decay_rate[None] * starts[:, None, None])
    before = jnp.concatenate([jnp.zeros_like(states[:1]), states[:-1]], axis=0) + carried
    earlier = jnp.sum(lead[None] * before[:, :, None, :], axis=1)
    return (inside + earlier).reshape(cap, width)


def out_kernel(g_ref, w_ref, t_ref, s_ref, m_ref, o_ref):
    acc = lax.dot_general(g_ref[...], w_ref[...], (((1,), (1,)), ((), ())), preferred_element_type=jnp.float32)
    res = t_ref[...].astype(jnp.float32) + acc + s_ref[...]
    o_ref[...] = jnp.where(m_ref[...] > 0, res, 0.0).astype(o_ref.dtype)

def project_out(gated, gathered, rows_in, steer, live, tile=4096):
    cap, slab = gated.shape
    width = rows_in.shape[1]
    tile = tile if width % tile == 0 else width
    column = (gathered.shape[1] - slab) // slab
    return pl.pallas_call(
        out_kernel,
        grid=(width // tile,),
        in_specs=[
            pl.BlockSpec((cap, slab), lambda j: (0, 0)),
            pl.BlockSpec((tile, slab), lambda j: (j, column)),
            pl.BlockSpec((cap, tile), lambda j: (0, j)),
            pl.BlockSpec((1, tile), lambda j: (0, j)),
            pl.BlockSpec((cap, 1), lambda j: (0, 0)),
        ],
        out_specs=pl.BlockSpec((cap, tile), lambda j: (0, j)),
        out_shape=jax.ShapeDtypeStruct((cap, width), rows_in.dtype),
        cost_estimate=pl.CostEstimate(flops=2 * cap * slab * width, transcendentals=0,
            bytes_accessed=2 * (cap * slab + width * slab + 2 * cap * width) + 4 * width),
    )(gated, gathered, rows_in, steer.reshape(1, width), live.astype(jnp.int32).reshape(cap, 1))

def per_device(
    tokens,
    lengths,
    norm_gain,
    w_in,
    short_filter,
    decay_rate,
    residue,
    skip_gain,
    w_out,
    steer_table,
    steer_layer,
    steer_slab,
):
    cap = tokens.shape[2]
    width = tokens.shape[3]
    slab = residue.shape[1]
    groups = lax.axis_size("ctx")
    rows_in = tokens.reshape(cap, width)
    normed = normalize(rows_in, norm_gain)
    position = lax.axis_index("ctx")
    group_lens = lengths.reshape(-1)
    own_len = lax.dynamic_index_in_dim(group_lens, position, 0, keepdims=False)
    live = jnp.arange(cap) < own_len
    own_tail = lax.dynamic_slice_in_dim(normed, own_len - 2, 2, 0)
    tail_normed = from_behind(own_tail, "ctx", 1)

    block = BLOCK if cap % BLOCK == 0 else cap
    toeplitz, lead, close = filter_tables(decay_rate, residue, block)

    lens_f = group_lens.astype(jnp.float32)
    cumlen = jnp.cumsum(lens_f)
    rescale = jnp.exp(decay_rate * (cap - own_len).astype(jnp.float32))

    piece = jnp.concatenate([w_in, w_out.T], axis=1)
    gathered = lax.all_gather(piece, "dp", axis=0, tiled=True)
    w_in_all = gathered[:, : 3 * slab]
    rows_ext = jnp.concatenate([tail_normed, normed], axis=0)
    extended = jnp.dot(rows_ext, w_in_all, preferred_element_type=jnp.float32)
    extended = lax.reduce_precision(extended, exponent_bits=8, mantissa_bits=7)
    feat = (
        short_filter[0] * extended[2:]
        + short_filter[1] * extended[1:-1]
        + short_filter[2] * extended[:-2]
    )
    gate = feat[:, :slab]
    drive = jnp.where(live[:, None], feat[:, slab : 2 * slab] * feat[:, 2 * slab :], 0.0)
    states = block_states(drive, decay_rate, close, block)
    ending = states[-1] * rescale
    incoming = jnp.zeros_like(ending)
    for k in range(1, groups):
        got = from_behind(ending, "ctx", k)
        source = position - k
        between = lax.dynamic_index_in_dim(
            cumlen, jnp.maximum(position - 1, 0), 0, keepdims=False
        ) - lax.dynamic_index_in_dim(cumlen, jnp.maximum(source, 0), 0, keepdims=False)
        weight = jnp.where(source >= 0, jnp.exp(-decay_rate * between), 0.0)
        incoming = incoming + weight * got
    local = block_outputs(drive, states, incoming, decay_rate, toeplitz, lead, block)
    filtered = local + skip_gain[None, :] * drive
    gated = jnp.where(live[:, None], gate * filtered, 0.0).astype(jnp.bfloat16)
    rows2 = lax.dynamic_index_in_dim(steer_table, steer_layer[0], 0, keepdims=False)
    shift_vec = rows2[0] - rows2[1]
    columns = jnp.arange(width) // STEER_W
    steer = jnp.where(columns == steer_slab[0], 2.0 * shift_vec, 0.0)
    result = project_out(gated, gathered, rows_in, steer, live)
    return result.reshape(tokens.shape)


def solution(mesh):
    placed = (
        P("dp", "ctx", None, None),
        P("dp", None),
        P(),
        P("dp", None),
        P(),
        P(),
        P(),
        P(),
        P(None, "dp"),
        P(),
        P("dp"),
        P("dp"),
    )
    return jax.shard_map(
        per_device,
        mesh=mesh,
        in_specs=placed,
        out_specs=P("dp", "ctx", None, None),
        check_vma=False,
    )
```

```python
import jax
import jax.numpy as jnp
from jax import lax
from jax.experimental import pallas as pl
from jax.sharding import PartitionSpec as P

STEER_W = 1024
BLOCK = 32


def from_behind(value, axis, steps):
    count = lax.axis_size(axis)
    first, last = (max(0, -steps), min(count, count - steps))
    return lax.ppermute(value, axis, [(source, source + steps) for source in range(first, last)])


def normalize(rows_in, gain):
    values = rows_in.astype(jnp.float32)
    scale = lax.rsqrt(jnp.mean(values * values, axis=1, keepdims=True) + 1e-06)
    return (values * scale * gain[None, :]).astype(jnp.bfloat16)


def filter_tables(decay_rate, residue, block):
    lags = jnp.arange(block)
    lags_float = lags.astype(jnp.float32)
    taps = jnp.sum(residue[None] * jnp.exp(-decay_rate[None] * lags_float[:, None, None]), axis=1)
    diff = lags[:, None] - lags[None, :]
    toeplitz = jnp.where((diff >= 0)[:, :, None], taps[jnp.clip(diff, 0, block - 1)], 0.0)
    toeplitz = jnp.transpose(toeplitz, (1, 0, 2))
    lead = residue[:, None] * jnp.exp(-decay_rate[:, None] * (lags_float + 1.0)[None, :, None])
    close = jnp.exp(-decay_rate[None] * (block - 1 - lags_float)[:, None, None])
    return toeplitz, lead, close


def block_states(drive, decay_rate, close, block):
    cap, width = drive.shape
    count = cap // block
    pieces = drive.reshape(count, block, width)
    ends = jnp.sum(close[None] * pieces[:, :, None, :], axis=1)
    steps = jnp.arange(count)
    gap = (steps[:, None] - steps[None, :]).astype(jnp.float32)
    powers = jnp.where(
        (gap >= 0)[:, :, None, None],
        jnp.exp(-decay_rate[None, None] * (block * jnp.maximum(gap, 0.0))[:, :, None, None]),
        0.0,
    )
    return jnp.sum(powers * ends[None], axis=1)


def block_outputs(drive, states, incoming, decay_rate, toeplitz, lead, block):
    cap, width = drive.shape
    count = cap // block
    pieces = drive.reshape(count, block, width)
    inside = jnp.sum(toeplitz[None] * pieces[:, :, None, :], axis=1)
    starts = (jnp.arange(count) * block).astype(jnp.float32)
    carried = incoming[None] * jnp.exp(-decay_rate[None] * starts[:, None, None])
    before = jnp.concatenate([jnp.zeros_like(states[:1]), states[:-1]], axis=0) + carried
    earlier = jnp.sum(lead[None] * before[:, :, None, :], axis=1)
    return (inside + earlier).reshape(cap, width)


def pack_kernel(wi_ref, wo_ref, o_ref):
    cols = wi_ref.shape[1]
    o_ref[:, :cols] = wi_ref[...]
    o_ref[:, cols:] = wo_ref[...].astype(jnp.float32).T.astype(o_ref.dtype)


def pack_weights(w_in, w_out):
    rows, cols = w_in.shape
    slab = w_out.shape[0]
    step = 256 if rows % 256 == 0 else rows
    return pl.pallas_call(
        pack_kernel,
        grid=(rows // step,),
        in_specs=[
            pl.BlockSpec((step, cols), lambda i: (i, 0)),
            pl.BlockSpec((slab, step), lambda i: (0, i)),
        ],
        out_specs=pl.BlockSpec((step, cols + slab), lambda i: (i, 0)),
        out_shape=jax.ShapeDtypeStruct((rows, cols + slab), w_in.dtype),
    )(w_in, w_out)

def out_kernel(g_ref, w_ref, t_ref, s_ref, m_ref, o_ref):
    acc = lax.dot_general(g_ref[...], w_ref[...], (((1,), (1,)), ((), ())), preferred_element_type=jnp.float32)
    res = t_ref[...].astype(jnp.float32) + acc + s_ref[...]
    o_ref[...] = jnp.where(m_ref[...] > 0, res, 0.0).astype(o_ref.dtype)

def project_out(gated, gathered, rows_in, steer, live, tile=4096):
    cap, slab = gated.shape
    width = rows_in.shape[1]
    tile = tile if width % tile == 0 else width
    column = (gathered.shape[1] - slab) // slab
    return pl.pallas_call(
        out_kernel,
        grid=(width // tile,),
        in_specs=[
            pl.BlockSpec((cap, slab), lambda j: (0, 0)),
            pl.BlockSpec((tile, slab), lambda j: (j, column)),
            pl.BlockSpec((cap, tile), lambda j: (0, j)),
            pl.BlockSpec((1, tile), lambda j: (0, j)),
            pl.BlockSpec((cap, 1), lambda j: (0, 0)),
        ],
        out_specs=pl.BlockSpec((cap, tile), lambda j: (0, j)),
        out_shape=jax.ShapeDtypeStruct((cap, width), rows_in.dtype),
        cost_estimate=pl.CostEstimate(flops=2 * cap * slab * width, transcendentals=0,
            bytes_accessed=2 * (cap * slab + width * slab + 2 * cap * width) + 4 * width),
    )(gated, gathered, rows_in, steer.reshape(1, width), live.astype(jnp.int32).reshape(cap, 1))

def per_device(
    tokens,
    lengths,
    norm_gain,
    w_in,
    short_filter,
    decay_rate,
    residue,
    skip_gain,
    w_out,
    steer_table,
    steer_layer,
    steer_slab,
):
    cap = tokens.shape[2]
    width = tokens.shape[3]
    slab = residue.shape[1]
    groups = lax.axis_size("ctx")
    rows_in = tokens.reshape(cap, width)
    normed = normalize(rows_in, norm_gain)
    position = lax.axis_index("ctx")
    group_lens = lengths.reshape(-1)
    own_len = lax.dynamic_index_in_dim(group_lens, position, 0, keepdims=False)
    live = jnp.arange(cap) < own_len
    own_tail = lax.dynamic_slice_in_dim(normed, own_len - 2, 2, 0)
    tail_normed = from_behind(own_tail, "ctx", 1)

    block = BLOCK if cap % BLOCK == 0 else cap
    toeplitz, lead, close = filter_tables(decay_rate, residue, block)

    lens_f = group_lens.astype(jnp.float32)
    cumlen = jnp.cumsum(lens_f)
    rescale = jnp.exp(decay_rate * (cap - own_len).astype(jnp.float32))

    piece = pack_weights(w_in, w_out)
    gathered = lax.all_gather(piece, "dp", axis=0, tiled=True)
    w_in_all = gathered[:, : 3 * slab]
    rows_ext = jnp.concatenate([tail_normed, normed], axis=0)
    extended = jnp.dot(rows_ext, w_in_all, preferred_element_type=jnp.float32)
    extended = lax.reduce_precision(extended, exponent_bits=8, mantissa_bits=7)
    feat = (
        short_filter[0] * extended[2:]
        + short_filter[1] * extended[1:-1]
        + short_filter[2] * extended[:-2]
    )
    gate = feat[:, :slab]
    drive = jnp.where(live[:, None], feat[:, slab : 2 * slab] * feat[:, 2 * slab :], 0.0)
    states = block_states(drive, decay_rate, close, block)
    ending = states[-1] * rescale
    incoming = jnp.zeros_like(ending)
    for k in range(1, groups):
        got = from_behind(ending, "ctx", k)
        source = position - k
        between = lax.dynamic_index_in_dim(
            cumlen, jnp.maximum(position - 1, 0), 0, keepdims=False
        ) - lax.dynamic_index_in_dim(cumlen, jnp.maximum(source, 0), 0, keepdims=False)
        weight = jnp.where(source >= 0, jnp.exp(-decay_rate * between), 0.0)
        incoming = incoming + weight * got
    local = block_outputs(drive, states, incoming, decay_rate, toeplitz, lead, block)
    filtered = local + skip_gain[None, :] * drive
    gated = jnp.where(live[:, None], gate * filtered, 0.0).astype(jnp.bfloat16)
    rows2 = lax.dynamic_index_in_dim(steer_table, steer_layer[0], 0, keepdims=False)
    shift_vec = rows2[0] - rows2[1]
    columns = jnp.arange(width) // STEER_W
    steer = jnp.where(columns == steer_slab[0], 2.0 * shift_vec, 0.0)
    result = project_out(gated, gathered, rows_in, steer, live)
    return result.reshape(tokens.shape)


def solution(mesh):
    placed = (
        P("dp", "ctx", None, None),
        P("dp", None),
        P(),
        P("dp", None),
        P(),
        P(),
        P(),
        P(),
        P(None, "dp"),
        P(),
        P("dp"),
        P("dp"),
    )
    return jax.shard_map(
        per_device,
        mesh=mesh,
        in_specs=placed,
        out_specs=P("dp", "ctx", None, None),
        check_vma=False,
    )
```

```python
import jax
import jax.numpy as jnp
from jax import lax
from jax.experimental import pallas as pl
from jax.experimental.pallas import tpu as pltpu
from jax.sharding import PartitionSpec as P

STEER_W = 1024
BLOCK = 32


def from_behind(value, axis, steps):
    count = lax.axis_size(axis)
    first, last = (max(0, -steps), min(count, count - steps))
    return lax.ppermute(value, axis, [(source, source + steps) for source in range(first, last)])


def normalize(rows_in, gain):
    values = rows_in.astype(jnp.float32)
    scale = lax.rsqrt(jnp.mean(values * values, axis=1, keepdims=True) + 1e-06)
    return (values * scale * gain[None, :]).astype(jnp.bfloat16)


def filter_tables(decay_rate, residue, block):
    lags = jnp.arange(block)
    lags_float = lags.astype(jnp.float32)
    taps = jnp.sum(residue[None] * jnp.exp(-decay_rate[None] * lags_float[:, None, None]), axis=1)
    diff = lags[:, None] - lags[None, :]
    toeplitz = jnp.where((diff >= 0)[:, :, None], taps[jnp.clip(diff, 0, block - 1)], 0.0)
    toeplitz = jnp.transpose(toeplitz, (1, 0, 2))
    lead = residue[:, None] * jnp.exp(-decay_rate[:, None] * (lags_float + 1.0)[None, :, None])
    close = jnp.exp(-decay_rate[None] * (block - 1 - lags_float)[:, None, None])
    return toeplitz, lead, close


def block_states(drive, decay_rate, close, block):
    cap, width = drive.shape
    count = cap // block
    pieces = drive.reshape(count, block, width)
    ends = jnp.sum(close[None] * pieces[:, :, None, :], axis=1)
    steps = jnp.arange(count)
    gap = (steps[:, None] - steps[None, :]).astype(jnp.float32)
    powers = jnp.where(
        (gap >= 0)[:, :, None, None],
        jnp.exp(-decay_rate[None, None] * (block * jnp.maximum(gap, 0.0))[:, :, None, None]),
        0.0,
    )
    return jnp.sum(powers * ends[None], axis=1)


def block_outputs(drive, states, incoming, decay_rate, toeplitz, lead, block):
    cap, width = drive.shape
    count = cap // block
    pieces = drive.reshape(count, block, width)
    inside = jnp.sum(toeplitz[None] * pieces[:, :, None, :], axis=1)
    starts = (jnp.arange(count) * block).astype(jnp.float32)
    carried = incoming[None] * jnp.exp(-decay_rate[None] * starts[:, None, None])
    before = jnp.concatenate([jnp.zeros_like(states[:1]), states[:-1]], axis=0) + carried
    earlier = jnp.sum(lead[None] * before[:, :, None, :], axis=1)
    return (inside + earlier).reshape(cap, width)


def pack_kernel(wi_ref, wo_ref, o_ref):
    cols = wi_ref.shape[1]
    o_ref[:, :cols] = wi_ref[...]
    o_ref[:, cols:] = wo_ref[...].astype(jnp.float32).T.astype(o_ref.dtype)


def pack_weights(w_in, w_out):
    rows, cols = w_in.shape
    slab = w_out.shape[0]
    step = 256 if rows % 256 == 0 else rows
    return pl.pallas_call(
        pack_kernel,
        grid=(rows // step,),
        in_specs=[
            pl.BlockSpec((step, cols), lambda i: (i, 0)),
            pl.BlockSpec((slab, step), lambda i: (0, i)),
        ],
        out_specs=pl.BlockSpec((step, cols + slab), lambda i: (i, 0)),
        out_shape=jax.ShapeDtypeStruct((rows, cols + slab), w_in.dtype),
    )(w_in, w_out)

def proj_kernel(x_ref, w_ref, o_ref):
    o_ref[...] = jnp.dot(x_ref[...], w_ref[...], preferred_element_type=jnp.float32).astype(
        o_ref.dtype
    )


def project_in(rows_ext, gathered, columns, tile=512):
    count, depth = rows_ext.shape
    tile = tile if columns % tile == 0 else columns
    return pl.pallas_call(
        proj_kernel,
        grid=(columns // tile,),
        in_specs=[
            pl.BlockSpec((count, depth), lambda j: (0, 0)),
            pl.BlockSpec((depth, tile), lambda j: (0, j)),
        ],
        out_specs=pl.BlockSpec((count, tile), lambda j: (0, j)),
        out_shape=jax.ShapeDtypeStruct((count, columns), jnp.bfloat16),
        compiler_params=pltpu.CompilerParams(vmem_limit_bytes=60 * 1024 * 1024),
        cost_estimate=pl.CostEstimate(
            flops=2 * count * depth * columns,
            transcendentals=0,
            bytes_accessed=2 * (count * depth + depth * columns + count * columns),
        ),
    )(rows_ext, gathered)


def out_kernel(g_ref, w_ref, t_ref, s_ref, m_ref, o_ref):
    acc = lax.dot_general(g_ref[...], w_ref[...], (((1,), (1,)), ((), ())), preferred_element_type=jnp.float32)
    res = t_ref[...].astype(jnp.float32) + acc + s_ref[...]
    o_ref[...] = jnp.where(m_ref[...] > 0, res, 0.0).astype(o_ref.dtype)

def project_out(gated, gathered, rows_in, steer, live, tile=4096):
    cap, slab = gated.shape
    width = rows_in.shape[1]
    tile = tile if width % tile == 0 else width
    column = (gathered.shape[1] - slab) // slab
    return pl.pallas_call(
        out_kernel,
        grid=(width // tile,),
        in_specs=[
            pl.BlockSpec((cap, slab), lambda j: (0, 0)),
            pl.BlockSpec((tile, slab), lambda j: (j, column)),
            pl.BlockSpec((cap, tile), lambda j: (0, j)),
            pl.BlockSpec((1, tile), lambda j: (0, j)),
            pl.BlockSpec((cap, 1), lambda j: (0, 0)),
        ],
        out_specs=pl.BlockSpec((cap, tile), lambda j: (0, j)),
        out_shape=jax.ShapeDtypeStruct((cap, width), rows_in.dtype),
        cost_estimate=pl.CostEstimate(flops=2 * cap * slab * width, transcendentals=0,
            bytes_accessed=2 * (cap * slab + width * slab + 2 * cap * width) + 4 * width),
    )(gated, gathered, rows_in, steer.reshape(1, width), live.astype(jnp.int32).reshape(cap, 1))

def per_device(
    tokens,
    lengths,
    norm_gain,
    w_in,
    short_filter,
    decay_rate,
    residue,
    skip_gain,
    w_out,
    steer_table,
    steer_layer,
    steer_slab,
):
    cap = tokens.shape[2]
    width = tokens.shape[3]
    slab = residue.shape[1]
    groups = lax.axis_size("ctx")
    rows_in = tokens.reshape(cap, width)
    normed = normalize(rows_in, norm_gain)
    position = lax.axis_index("ctx")
    group_lens = lengths.reshape(-1)
    own_len = lax.dynamic_index_in_dim(group_lens, position, 0, keepdims=False)
    live = jnp.arange(cap) < own_len
    own_tail = lax.dynamic_slice_in_dim(normed, own_len - 2, 2, 0)
    tail_normed = from_behind(own_tail, "ctx", 1)

    block = BLOCK if cap % BLOCK == 0 else cap
    toeplitz, lead, close = filter_tables(decay_rate, residue, block)

    lens_f = group_lens.astype(jnp.float32)
    cumlen = jnp.cumsum(lens_f)
    rescale = jnp.exp(decay_rate * (cap - own_len).astype(jnp.float32))

    piece = pack_weights(w_in, w_out)
    gathered = lax.all_gather(piece, "dp", axis=0, tiled=True)
    rows_ext = jnp.concatenate([tail_normed, normed], axis=0)
    extended = project_in(rows_ext, gathered, 3 * slab).astype(jnp.float32)
    feat = (
        short_filter[0] * extended[2:]
        + short_filter[1] * extended[1:-1]
        + short_filter[2] * extended[:-2]
    )
    gate = feat[:, :slab]
    drive = jnp.where(live[:, None], feat[:, slab : 2 * slab] * feat[:, 2 * slab :], 0.0)
    states = block_states(drive, decay_rate, close, block)
    ending = states[-1] * rescale
    incoming = jnp.zeros_like(ending)
    for k in range(1, groups):
        got = from_behind(ending, "ctx", k)
        source = position - k
        between = lax.dynamic_index_in_dim(
            cumlen, jnp.maximum(position - 1, 0), 0, keepdims=False
        ) - lax.dynamic_index_in_dim(cumlen, jnp.maximum(source, 0), 0, keepdims=False)
        weight = jnp.where(source >= 0, jnp.exp(-decay_rate * between), 0.0)
        incoming = incoming + weight * got
    local = block_outputs(drive, states, incoming, decay_rate, toeplitz, lead, block)
    filtered = local + skip_gain[None, :] * drive
    gated = jnp.where(live[:, None], gate * filtered, 0.0).astype(jnp.bfloat16)
    rows2 = lax.dynamic_index_in_dim(steer_table, steer_layer[0], 0, keepdims=False)
    shift_vec = rows2[0] - rows2[1]
    columns = jnp.arange(width) // STEER_W
    steer = jnp.where(columns == steer_slab[0], 2.0 * shift_vec, 0.0)
    result = project_out(gated, gathered, rows_in, steer, live)
    return result.reshape(tokens.shape)


def solution(mesh):
    placed = (
        P("dp", "ctx", None, None),
        P("dp", None),
        P(),
        P("dp", None),
        P(),
        P(),
        P(),
        P(),
        P(None, "dp"),
        P(),
        P("dp"),
        P("dp"),
    )
    return jax.shard_map(
        per_device,
        mesh=mesh,
        in_specs=placed,
        out_specs=P("dp", "ctx", None, None),
        check_vma=False,
    )
```

```python
import jax
import jax.numpy as jnp
from jax import lax
from jax.experimental import pallas as pl
from jax.sharding import PartitionSpec as P

STEER_W = 1024
BLOCK = 32


def from_behind(value, axis, steps):
    count = lax.axis_size(axis)
    first, last = (max(0, -steps), min(count, count - steps))
    return lax.ppermute(value, axis, [(source, source + steps) for source in range(first, last)])


def normalize(rows_in, gain):
    values = rows_in.astype(jnp.float32)
    scale = lax.rsqrt(jnp.mean(values * values, axis=1, keepdims=True) + 1e-06)
    return (values * scale * gain[None, :]).astype(jnp.bfloat16)


def filter_tables(decay_rate, residue, block):
    lags = jnp.arange(block)
    lags_float = lags.astype(jnp.float32)
    taps = jnp.sum(residue[None] * jnp.exp(-decay_rate[None] * lags_float[:, None, None]), axis=1)
    diff = lags[:, None] - lags[None, :]
    toeplitz = jnp.where((diff >= 0)[:, :, None], taps[jnp.clip(diff, 0, block - 1)], 0.0)
    toeplitz = jnp.transpose(toeplitz, (1, 0, 2))
    lead = residue[:, None] * jnp.exp(-decay_rate[:, None] * (lags_float + 1.0)[None, :, None])
    close = jnp.exp(-decay_rate[None] * (block - 1 - lags_float)[:, None, None])
    return toeplitz, lead, close


def block_states(drive, decay_rate, close, block):
    cap, width = drive.shape
    count = cap // block
    pieces = drive.reshape(count, block, width)
    ends = jnp.sum(close[None] * pieces[:, :, None, :], axis=1)
    steps = jnp.arange(count)
    gap = (steps[:, None] - steps[None, :]).astype(jnp.float32)
    powers = jnp.where(
        (gap >= 0)[:, :, None, None],
        jnp.exp(-decay_rate[None, None] * (block * jnp.maximum(gap, 0.0))[:, :, None, None]),
        0.0,
    )
    return jnp.sum(powers * ends[None], axis=1)


def block_outputs(drive, states, incoming, decay_rate, toeplitz, lead, block):
    cap, width = drive.shape
    count = cap // block
    pieces = drive.reshape(count, block, width)
    inside = jnp.sum(toeplitz[None] * pieces[:, :, None, :], axis=1)
    starts = (jnp.arange(count) * block).astype(jnp.float32)
    carried = incoming[None] * jnp.exp(-decay_rate[None] * starts[:, None, None])
    before = jnp.concatenate([jnp.zeros_like(states[:1]), states[:-1]], axis=0) + carried
    earlier = jnp.sum(lead[None] * before[:, :, None, :], axis=1)
    return (inside + earlier).reshape(cap, width)


def pack_kernel(wi_ref, wo_ref, o_ref):
    cols = wi_ref.shape[1]
    o_ref[:, :cols] = wi_ref[...]
    o_ref[:, cols:] = wo_ref[...].astype(jnp.float32).T.astype(o_ref.dtype)


def pack_weights(w_in, w_out):
    rows, cols = w_in.shape
    slab = w_out.shape[0]
    step = 256 if rows % 256 == 0 else rows
    return pl.pallas_call(
        pack_kernel,
        grid=(rows // step,),
        in_specs=[
            pl.BlockSpec((step, cols), lambda i: (i, 0)),
            pl.BlockSpec((slab, step), lambda i: (0, i)),
        ],
        out_specs=pl.BlockSpec((step, cols + slab), lambda i: (i, 0)),
        out_shape=jax.ShapeDtypeStruct((rows, cols + slab), w_in.dtype),
    )(w_in, w_out)

def out_kernel(gate_ref, local_ref, drive_ref, skip_ref, w_ref, t_ref, s_ref, m_ref, o_ref):
    alive = m_ref[...] > 0
    filtered = local_ref[...] + skip_ref[...] * drive_ref[...]
    gated = jnp.where(alive, gate_ref[...] * filtered, 0.0).astype(w_ref.dtype)
    acc = lax.dot_general(gated, w_ref[...], (((1,), (1,)), ((), ())), preferred_element_type=jnp.float32)
    res = t_ref[...].astype(jnp.float32) + acc + s_ref[...]
    o_ref[...] = jnp.where(alive, res, 0.0).astype(o_ref.dtype)


def project_out(gate, local, drive, skip, gathered, rows_in, steer, live, tile=4096):
    cap, slab = gate.shape
    width = rows_in.shape[1]
    tile = tile if width % tile == 0 else width
    column = (gathered.shape[1] - slab) // slab
    whole = pl.BlockSpec((cap, slab), lambda j: (0, 0))
    return pl.pallas_call(
        out_kernel,
        grid=(width // tile,),
        in_specs=[
            whole,
            whole,
            whole,
            pl.BlockSpec((1, slab), lambda j: (0, 0)),
            pl.BlockSpec((tile, slab), lambda j: (j, column)),
            pl.BlockSpec((cap, tile), lambda j: (0, j)),
            pl.BlockSpec((1, tile), lambda j: (0, j)),
            pl.BlockSpec((cap, 1), lambda j: (0, 0)),
        ],
        out_specs=pl.BlockSpec((cap, tile), lambda j: (0, j)),
        out_shape=jax.ShapeDtypeStruct((cap, width), rows_in.dtype),
        cost_estimate=pl.CostEstimate(flops=2 * cap * slab * width, transcendentals=0,
            bytes_accessed=12 * cap * slab + 2 * (width * slab + 2 * cap * width) + 4 * width),
    )(gate, local, drive, skip.reshape(1, slab), gathered, rows_in, steer.reshape(1, width),
      live.astype(jnp.int32).reshape(cap, 1))


def per_device(
    tokens,
    lengths,
    norm_gain,
    w_in,
    short_filter,
    decay_rate,
    residue,
    skip_gain,
    w_out,
    steer_table,
    steer_layer,
    steer_slab,
):
    cap = tokens.shape[2]
    width = tokens.shape[3]
    slab = residue.shape[1]
    groups = lax.axis_size("ctx")
    rows_in = tokens.reshape(cap, width)
    normed = normalize(rows_in, norm_gain)
    position = lax.axis_index("ctx")
    group_lens = lengths.reshape(-1)
    own_len = lax.dynamic_index_in_dim(group_lens, position, 0, keepdims=False)
    live = jnp.arange(cap) < own_len
    own_tail = lax.dynamic_slice_in_dim(normed, own_len - 2, 2, 0)
    tail_normed = from_behind(own_tail, "ctx", 1)

    block = BLOCK if cap % BLOCK == 0 else cap
    toeplitz, lead, close = filter_tables(decay_rate, residue, block)

    lens_f = group_lens.astype(jnp.float32)
    cumlen = jnp.cumsum(lens_f)
    rescale = jnp.exp(decay_rate * (cap - own_len).astype(jnp.float32))

    piece = pack_weights(w_in, w_out)
    gathered = lax.all_gather(piece, "dp", axis=0, tiled=True)
    w_in_all = gathered[:, : 3 * slab]
    rows_ext = jnp.concatenate([tail_normed, normed], axis=0)
    extended = jnp.dot(rows_ext, w_in_all, preferred_element_type=jnp.float32)
    extended = lax.reduce_precision(extended, exponent_bits=8, mantissa_bits=7)
    feat = (
        short_filter[0] * extended[2:]
        + short_filter[1] * extended[1:-1]
        + short_filter[2] * extended[:-2]
    )
    gate = feat[:, :slab]
    drive = jnp.where(live[:, None], feat[:, slab : 2 * slab] * feat[:, 2 * slab :], 0.0)
    states = block_states(drive, decay_rate, close, block)
    ending = states[-1] * rescale
    incoming = jnp.zeros_like(ending)
    for k in range(1, groups):
        got = from_behind(ending, "ctx", k)
        source = position - k
        between = lax.dynamic_index_in_dim(
            cumlen, jnp.maximum(position - 1, 0), 0, keepdims=False
        ) - lax.dynamic_index_in_dim(cumlen, jnp.maximum(source, 0), 0, keepdims=False)
        weight = jnp.where(source >= 0, jnp.exp(-decay_rate * between), 0.0)
        incoming = incoming + weight * got
    local = block_outputs(drive, states, incoming, decay_rate, toeplitz, lead, block)
    rows2 = lax.dynamic_index_in_dim(steer_table, steer_layer[0], 0, keepdims=False)
    shift_vec = rows2[0] - rows2[1]
    columns = jnp.arange(width) // STEER_W
    steer = jnp.where(columns == steer_slab[0], 2.0 * shift_vec, 0.0)
    result = project_out(gate, local, drive, skip_gain, gathered, rows_in, steer, live)
    return result.reshape(tokens.shape)


def solution(mesh):
    placed = (
        P("dp", "ctx", None, None),
        P("dp", None),
        P(),
        P("dp", None),
        P(),
        P(),
        P(),
        P(),
        P(None, "dp"),
        P(),
        P("dp"),
        P("dp"),
    )
    return jax.shard_map(
        per_device,
        mesh=mesh,
        in_specs=placed,
        out_specs=P("dp", "ctx", None, None),
        check_vma=False,
    )
```

```python
import jax
import jax.numpy as jnp
from jax import lax
from jax.experimental import pallas as pl
from jax.sharding import PartitionSpec as P

STEER_W = 1024
BLOCK = 32


def from_behind(value, axis, steps):
    count = lax.axis_size(axis)
    first, last = (max(0, -steps), min(count, count - steps))
    return lax.ppermute(value, axis, [(source, source + steps) for source in range(first, last)])


def normalize(rows_in, gain):
    values = rows_in.astype(jnp.float32)
    scale = lax.rsqrt(jnp.mean(values * values, axis=1, keepdims=True) + 1e-06)
    return (values * scale * gain[None, :]).astype(jnp.bfloat16)


def filter_tables(decay_rate, residue, block):
    lags = jnp.arange(block)
    lags_float = lags.astype(jnp.float32)
    taps = jnp.sum(residue[None] * jnp.exp(-decay_rate[None] * lags_float[:, None, None]), axis=1)
    diff = lags[:, None] - lags[None, :]
    toeplitz = jnp.where((diff >= 0)[:, :, None], taps[jnp.clip(diff, 0, block - 1)], 0.0)
    toeplitz = jnp.transpose(toeplitz, (1, 0, 2))
    lead = residue[:, None] * jnp.exp(-decay_rate[:, None] * (lags_float + 1.0)[None, :, None])
    close = jnp.exp(-decay_rate[None] * (block - 1 - lags_float)[:, None, None])
    return toeplitz, lead, close


def block_powers(decay_rate, count, block):
    steps = jnp.arange(count)
    gap = (steps[:, None] - steps[None, :]).astype(jnp.float32)
    return jnp.where(
        (gap >= 0)[:, :, None, None],
        jnp.exp(-decay_rate[None, None] * (block * jnp.maximum(gap, 0.0))[:, :, None, None]),
        0.0,
    )


def block_states(drive, powers, close, block):
    cap, width = drive.shape
    pieces = drive.reshape(cap // block, block, width)
    ends = jnp.sum(close[None] * pieces[:, :, None, :], axis=1)
    return jnp.sum(powers * ends[None], axis=1)


def block_outputs(drive, states, incoming, decay_rate, toeplitz, lead, block):
    cap, width = drive.shape
    count = cap // block
    pieces = drive.reshape(count, block, width)
    inside = jnp.sum(toeplitz[None] * pieces[:, :, None, :], axis=1)
    starts = (jnp.arange(count) * block).astype(jnp.float32)
    carried = incoming[None] * jnp.exp(-decay_rate[None] * starts[:, None, None])
    before = jnp.concatenate([jnp.zeros_like(states[:1]), states[:-1]], axis=0) + carried
    earlier = jnp.sum(lead[None] * before[:, :, None, :], axis=1)
    return (inside + earlier).reshape(cap, width)


def pack_kernel(wi_ref, wo_ref, o_ref):
    cols = wi_ref.shape[1]
    o_ref[:, :cols] = wi_ref[...]
    o_ref[:, cols:] = wo_ref[...].astype(jnp.float32).T.astype(o_ref.dtype)


def pack_weights(w_in, w_out):
    rows, cols = w_in.shape
    slab = w_out.shape[0]
    step = 256 if rows % 256 == 0 else rows
    return pl.pallas_call(
        pack_kernel,
        grid=(rows // step,),
        in_specs=[
            pl.BlockSpec((step, cols), lambda i: (i, 0)),
            pl.BlockSpec((slab, step), lambda i: (0, i)),
        ],
        out_specs=pl.BlockSpec((step, cols + slab), lambda i: (i, 0)),
        out_shape=jax.ShapeDtypeStruct((rows, cols + slab), w_in.dtype),
    )(w_in, w_out)

def out_kernel(g_ref, w_ref, t_ref, s_ref, m_ref, o_ref):
    acc = lax.dot_general(g_ref[...], w_ref[...], (((1,), (1,)), ((), ())), preferred_element_type=jnp.float32)
    res = t_ref[...].astype(jnp.float32) + acc + s_ref[...]
    o_ref[...] = jnp.where(m_ref[...] > 0, res, 0.0).astype(o_ref.dtype)

def project_out(gated, gathered, rows_in, steer, live, tile=4096):
    cap, slab = gated.shape
    width = rows_in.shape[1]
    tile = tile if width % tile == 0 else width
    column = (gathered.shape[1] - slab) // slab
    return pl.pallas_call(
        out_kernel,
        grid=(width // tile,),
        in_specs=[
            pl.BlockSpec((cap, slab), lambda j: (0, 0)),
            pl.BlockSpec((tile, slab), lambda j: (j, column)),
            pl.BlockSpec((cap, tile), lambda j: (0, j)),
            pl.BlockSpec((1, tile), lambda j: (0, j)),
            pl.BlockSpec((cap, 1), lambda j: (0, 0)),
        ],
        out_specs=pl.BlockSpec((cap, tile), lambda j: (0, j)),
        out_shape=jax.ShapeDtypeStruct((cap, width), rows_in.dtype),
        cost_estimate=pl.CostEstimate(flops=2 * cap * slab * width, transcendentals=0,
            bytes_accessed=2 * (cap * slab + width * slab + 2 * cap * width) + 4 * width),
    )(gated, gathered, rows_in, steer.reshape(1, width), live.astype(jnp.int32).reshape(cap, 1))

def per_device(
    tokens,
    lengths,
    norm_gain,
    w_in,
    short_filter,
    decay_rate,
    residue,
    skip_gain,
    w_out,
    steer_table,
    steer_layer,
    steer_slab,
):
    cap = tokens.shape[2]
    width = tokens.shape[3]
    slab = residue.shape[1]
    groups = lax.axis_size("ctx")
    rows_in = tokens.reshape(cap, width)
    normed = normalize(rows_in, norm_gain)
    position = lax.axis_index("ctx")
    group_lens = lengths.reshape(-1)
    own_len = lax.dynamic_index_in_dim(group_lens, position, 0, keepdims=False)
    live = jnp.arange(cap) < own_len
    own_tail = lax.dynamic_slice_in_dim(normed, own_len - 2, 2, 0)
    tail_normed = from_behind(own_tail, "ctx", 1)

    block = BLOCK if cap % BLOCK == 0 else cap
    toeplitz, lead, close = filter_tables(decay_rate, residue, block)

    lens_f = group_lens.astype(jnp.float32)
    cumlen = jnp.cumsum(lens_f)
    rescale = jnp.exp(decay_rate * (cap - own_len).astype(jnp.float32))

    piece = pack_weights(w_in, w_out)
    gathered = lax.all_gather(piece, "dp", axis=0, tiled=True)
    w_in_all = gathered[:, : 3 * slab]
    rows_ext = jnp.concatenate([tail_normed, normed], axis=0)
    powers = block_powers(decay_rate, cap // block, block)
    rows_ext, powers = lax.optimization_barrier((rows_ext, powers))
    extended = jnp.dot(rows_ext, w_in_all, preferred_element_type=jnp.float32)
    extended = lax.reduce_precision(extended, exponent_bits=8, mantissa_bits=7)
    feat = (
        short_filter[0] * extended[2:]
        + short_filter[1] * extended[1:-1]
        + short_filter[2] * extended[:-2]
    )
    gate = feat[:, :slab]
    drive = jnp.where(live[:, None], feat[:, slab : 2 * slab] * feat[:, 2 * slab :], 0.0)
    states = block_states(drive, powers, close, block)
    ending = states[-1] * rescale
    incoming = jnp.zeros_like(ending)
    for k in range(1, groups):
        got = from_behind(ending, "ctx", k)
        source = position - k
        between = lax.dynamic_index_in_dim(
            cumlen, jnp.maximum(position - 1, 0), 0, keepdims=False
        ) - lax.dynamic_index_in_dim(cumlen, jnp.maximum(source, 0), 0, keepdims=False)
        weight = jnp.where(source >= 0, jnp.exp(-decay_rate * between), 0.0)
        incoming = incoming + weight * got
    local = block_outputs(drive, states, incoming, decay_rate, toeplitz, lead, block)
    filtered = local + skip_gain[None, :] * drive
    gated = jnp.where(live[:, None], gate * filtered, 0.0).astype(jnp.bfloat16)
    rows2 = lax.dynamic_index_in_dim(steer_table, steer_layer[0], 0, keepdims=False)
    shift_vec = rows2[0] - rows2[1]
    columns = jnp.arange(width) // STEER_W
    steer = jnp.where(columns == steer_slab[0], 2.0 * shift_vec, 0.0)
    result = project_out(gated, gathered, rows_in, steer, live)
    return result.reshape(tokens.shape)


def solution(mesh):
    placed = (
        P("dp", "ctx", None, None),
        P("dp", None),
        P(),
        P("dp", None),
        P(),
        P(),
        P(),
        P(),
        P(None, "dp"),
        P(),
        P("dp"),
        P("dp"),
    )
    return jax.shard_map(
        per_device,
        mesh=mesh,
        in_specs=placed,
        out_specs=P("dp", "ctx", None, None),
        check_vma=False,
    )
```

```python
import jax
import jax.numpy as jnp
from jax import lax
from jax.experimental import pallas as pl
from jax.sharding import PartitionSpec as P

STEER_W = 1024
BLOCK = 32


def from_behind(value, axis, steps):
    count = lax.axis_size(axis)
    first, last = (max(0, -steps), min(count, count - steps))
    return lax.ppermute(value, axis, [(source, source + steps) for source in range(first, last)])


def normalize(rows_in, gain):
    values = rows_in.astype(jnp.float32)
    scale = lax.rsqrt(jnp.mean(values * values, axis=1, keepdims=True) + 1e-06)
    return (values * scale * gain[None, :]).astype(jnp.bfloat16)


def filter_tables(decay_rate, residue, block):
    lags = jnp.arange(block)
    lags_float = lags.astype(jnp.float32)
    taps = jnp.sum(residue[None] * jnp.exp(-decay_rate[None] * lags_float[:, None, None]), axis=1)
    diff = lags[:, None] - lags[None, :]
    toeplitz = jnp.where((diff >= 0)[:, :, None], taps[jnp.clip(diff, 0, block - 1)], 0.0)
    toeplitz = jnp.transpose(toeplitz, (1, 0, 2))
    lead = residue[:, None] * jnp.exp(-decay_rate[:, None] * (lags_float + 1.0)[None, :, None])
    close = jnp.exp(-decay_rate[None] * (block - 1 - lags_float)[:, None, None])
    return toeplitz, lead, close


def block_powers(decay_rate, count, block):
    steps = jnp.arange(count)
    gap = (steps[:, None] - steps[None, :]).astype(jnp.float32)
    return jnp.where(
        (gap >= 0)[:, :, None, None],
        jnp.exp(-decay_rate[None, None] * (block * jnp.maximum(gap, 0.0))[:, :, None, None]),
        0.0,
    )


def block_states(drive, powers, close, block):
    cap, width = drive.shape
    pieces = drive.reshape(cap // block, block, width)
    ends = jnp.sum(close[None] * pieces[:, :, None, :], axis=1)
    return jnp.sum(powers * ends[None], axis=1)


def block_outputs(drive, states, incoming, reach, toeplitz, lead, block):
    cap, width = drive.shape
    count = cap // block
    pieces = drive.reshape(count, block, width)
    inside = jnp.sum(toeplitz[None] * pieces[:, :, None, :], axis=1)
    carried = incoming[None] * reach
    before = jnp.concatenate([jnp.zeros_like(states[:1]), states[:-1]], axis=0) + carried
    earlier = jnp.sum(lead[None] * before[:, :, None, :], axis=1)
    return (inside + earlier).reshape(cap, width)


def pack_kernel(wi_ref, wo_ref, o_ref):
    cols = wi_ref.shape[1]
    o_ref[:, :cols] = wi_ref[...]
    o_ref[:, cols:] = wo_ref[...].astype(jnp.float32).T.astype(o_ref.dtype)


def pack_weights(w_in, w_out):
    rows, cols = w_in.shape
    slab = w_out.shape[0]
    step = 256 if rows % 256 == 0 else rows
    return pl.pallas_call(
        pack_kernel,
        grid=(rows // step,),
        in_specs=[
            pl.BlockSpec((step, cols), lambda i: (i, 0)),
            pl.BlockSpec((slab, step), lambda i: (0, i)),
        ],
        out_specs=pl.BlockSpec((step, cols + slab), lambda i: (i, 0)),
        out_shape=jax.ShapeDtypeStruct((rows, cols + slab), w_in.dtype),
    )(w_in, w_out)

def out_kernel(g_ref, w_ref, t_ref, s_ref, m_ref, o_ref):
    acc = lax.dot_general(g_ref[...], w_ref[...], (((1,), (1,)), ((), ())), preferred_element_type=jnp.float32)
    res = t_ref[...].astype(jnp.float32) + acc + s_ref[...]
    o_ref[...] = jnp.where(m_ref[...] > 0, res, 0.0).astype(o_ref.dtype)

def project_out(gated, gathered, rows_in, steer, live, tile=4096):
    cap, slab = gated.shape
    width = rows_in.shape[1]
    tile = tile if width % tile == 0 else width
    column = (gathered.shape[1] - slab) // slab
    return pl.pallas_call(
        out_kernel,
        grid=(width // tile,),
        in_specs=[
            pl.BlockSpec((cap, slab), lambda j: (0, 0)),
            pl.BlockSpec((tile, slab), lambda j: (j, column)),
            pl.BlockSpec((cap, tile), lambda j: (0, j)),
            pl.BlockSpec((1, tile), lambda j: (0, j)),
            pl.BlockSpec((cap, 1), lambda j: (0, 0)),
        ],
        out_specs=pl.BlockSpec((cap, tile), lambda j: (0, j)),
        out_shape=jax.ShapeDtypeStruct((cap, width), rows_in.dtype),
        cost_estimate=pl.CostEstimate(flops=2 * cap * slab * width, transcendentals=0,
            bytes_accessed=2 * (cap * slab + width * slab + 2 * cap * width) + 4 * width),
    )(gated, gathered, rows_in, steer.reshape(1, width), live.astype(jnp.int32).reshape(cap, 1))

def per_device(
    tokens,
    lengths,
    norm_gain,
    w_in,
    short_filter,
    decay_rate,
    residue,
    skip_gain,
    w_out,
    steer_table,
    steer_layer,
    steer_slab,
):
    cap = tokens.shape[2]
    width = tokens.shape[3]
    slab = residue.shape[1]
    groups = lax.axis_size("ctx")
    rows_in = tokens.reshape(cap, width)
    normed = normalize(rows_in, norm_gain)
    position = lax.axis_index("ctx")
    group_lens = lengths.reshape(-1)
    own_len = lax.dynamic_index_in_dim(group_lens, position, 0, keepdims=False)
    live = jnp.arange(cap) < own_len
    own_tail = lax.dynamic_slice_in_dim(normed, own_len - 2, 2, 0)
    tail_normed = from_behind(own_tail, "ctx", 1)

    block = BLOCK if cap % BLOCK == 0 else cap
    toeplitz, lead, close = filter_tables(decay_rate, residue, block)

    lens_f = group_lens.astype(jnp.float32)
    cumlen = jnp.cumsum(lens_f)
    rescale = jnp.exp(decay_rate * (cap - own_len).astype(jnp.float32))

    piece = pack_weights(w_in, w_out)
    gathered = lax.all_gather(piece, "dp", axis=0, tiled=True)
    w_in_all = gathered[:, : 3 * slab]
    rows_ext = jnp.concatenate([tail_normed, normed], axis=0)
    powers = block_powers(decay_rate, cap // block, block)
    starts = (jnp.arange(cap // block) * block).astype(jnp.float32)
    reach = jnp.exp(-decay_rate[None] * starts[:, None, None])
    rows_ext, powers, reach = lax.optimization_barrier((rows_ext, powers, reach))
    extended = jnp.dot(rows_ext, w_in_all, preferred_element_type=jnp.float32)
    extended = lax.reduce_precision(extended, exponent_bits=8, mantissa_bits=7)
    feat = (
        short_filter[0] * extended[2:]
        + short_filter[1] * extended[1:-1]
        + short_filter[2] * extended[:-2]
    )
    gate = feat[:, :slab]
    drive = jnp.where(live[:, None], feat[:, slab : 2 * slab] * feat[:, 2 * slab :], 0.0)
    states = block_states(drive, powers, close, block)
    ending = states[-1] * rescale
    incoming = jnp.zeros_like(ending)
    for k in range(1, groups):
        got = from_behind(ending, "ctx", k)
        source = position - k
        between = lax.dynamic_index_in_dim(
            cumlen, jnp.maximum(position - 1, 0), 0, keepdims=False
        ) - lax.dynamic_index_in_dim(cumlen, jnp.maximum(source, 0), 0, keepdims=False)
        weight = jnp.where(source >= 0, jnp.exp(-decay_rate * between), 0.0)
        incoming = incoming + weight * got
    local = block_outputs(drive, states, incoming, reach, toeplitz, lead, block)
    filtered = local + skip_gain[None, :] * drive
    gated = jnp.where(live[:, None], gate * filtered, 0.0).astype(jnp.bfloat16)
    rows2 = lax.dynamic_index_in_dim(steer_table, steer_layer[0], 0, keepdims=False)
    shift_vec = rows2[0] - rows2[1]
    columns = jnp.arange(width) // STEER_W
    steer = jnp.where(columns == steer_slab[0], 2.0 * shift_vec, 0.0)
    result = project_out(gated, gathered, rows_in, steer, live)
    return result.reshape(tokens.shape)


def solution(mesh):
    placed = (
        P("dp", "ctx", None, None),
        P("dp", None),
        P(),
        P("dp", None),
        P(),
        P(),
        P(),
        P(),
        P(None, "dp"),
        P(),
        P("dp"),
        P("dp"),
    )
    return jax.shard_map(
        per_device,
        mesh=mesh,
        in_specs=placed,
        out_specs=P("dp", "ctx", None, None),
        check_vma=False,
    )
```

```python
import jax
import jax.numpy as jnp
from jax import lax
from jax.experimental import pallas as pl
from jax.sharding import PartitionSpec as P

STEER_W = 1024
BLOCK = 32


def from_behind(value, axis, steps):
    count = lax.axis_size(axis)
    first, last = (max(0, -steps), min(count, count - steps))
    return lax.ppermute(value, axis, [(source, source + steps) for source in range(first, last)])


def normalize(rows_in, gain):
    values = rows_in.astype(jnp.float32)
    scale = lax.rsqrt(jnp.mean(values * values, axis=1, keepdims=True) + 1e-06)
    return (values * scale * gain[None, :]).astype(jnp.bfloat16)


def filter_tables(decay_rate, residue, block):
    lags = jnp.arange(block)
    lags_float = lags.astype(jnp.float32)
    taps = jnp.sum(residue[None] * jnp.exp(-decay_rate[None] * lags_float[:, None, None]), axis=1)
    diff = lags[:, None] - lags[None, :]
    toeplitz = jnp.where((diff >= 0)[:, :, None], taps[jnp.clip(diff, 0, block - 1)], 0.0)
    toeplitz = jnp.transpose(toeplitz, (1, 0, 2))
    lead = residue[:, None] * jnp.exp(-decay_rate[:, None] * (lags_float + 1.0)[None, :, None])
    close = jnp.exp(-decay_rate[None] * (block - 1 - lags_float)[:, None, None])
    return toeplitz, lead, close


def block_powers(decay_rate, count, block):
    steps = jnp.arange(count)
    gap = (steps[:, None] - steps[None, :]).astype(jnp.float32)
    return jnp.where(
        (gap >= 0)[:, :, None, None],
        jnp.exp(-decay_rate[None, None] * (block * jnp.maximum(gap, 0.0))[:, :, None, None]),
        0.0,
    )


def block_states(drive, powers, close, block):
    cap, width = drive.shape
    pieces = drive.reshape(cap // block, block, width)
    ends = jnp.sum(close[None] * pieces[:, :, None, :], axis=1)
    return jnp.sum(powers * ends[None], axis=1)


def block_outputs(drive, states, incoming, reach, toeplitz, lead, block):
    cap, width = drive.shape
    count = cap // block
    pieces = drive.reshape(count, block, width)
    inside = jnp.sum(toeplitz[None] * pieces[:, :, None, :], axis=1)
    carried = incoming[None] * reach
    before = jnp.concatenate([jnp.zeros_like(states[:1]), states[:-1]], axis=0) + carried
    earlier = jnp.sum(lead[None] * before[:, :, None, :], axis=1)
    return (inside + earlier).reshape(cap, width)


def pack_kernel(wi_ref, wo_ref, o_ref):
    cols = wi_ref.shape[1]
    o_ref[:, :cols] = wi_ref[...]
    o_ref[:, cols:] = wo_ref[...].astype(jnp.float32).T.astype(o_ref.dtype)


def pack_weights(w_in, w_out):
    rows, cols = w_in.shape
    slab = w_out.shape[0]
    step = 256 if rows % 256 == 0 else rows
    return pl.pallas_call(
        pack_kernel,
        grid=(rows // step,),
        in_specs=[
            pl.BlockSpec((step, cols), lambda i: (i, 0)),
            pl.BlockSpec((slab, step), lambda i: (0, i)),
        ],
        out_specs=pl.BlockSpec((step, cols + slab), lambda i: (i, 0)),
        out_shape=jax.ShapeDtypeStruct((rows, cols + slab), w_in.dtype),
    )(w_in, w_out)

def out_kernel(g_ref, w_ref, t_ref, s_ref, m_ref, o_ref):
    acc = lax.dot_general(g_ref[...], w_ref[...], (((1,), (1,)), ((), ())), preferred_element_type=jnp.float32)
    res = t_ref[...].astype(jnp.float32) + acc + s_ref[...]
    o_ref[...] = jnp.where(m_ref[...] > 0, res, 0.0).astype(o_ref.dtype)

def project_out(gated, gathered, rows_in, steer, live, tile=4096):
    cap, slab = gated.shape
    width = rows_in.shape[1]
    tile = tile if width % tile == 0 else width
    column = (gathered.shape[1] - slab) // slab
    return pl.pallas_call(
        out_kernel,
        grid=(width // tile,),
        in_specs=[
            pl.BlockSpec((cap, slab), lambda j: (0, 0)),
            pl.BlockSpec((tile, slab), lambda j: (j, column)),
            pl.BlockSpec((cap, tile), lambda j: (0, j)),
            pl.BlockSpec((1, tile), lambda j: (0, j)),
            pl.BlockSpec((cap, 1), lambda j: (0, 0)),
        ],
        out_specs=pl.BlockSpec((cap, tile), lambda j: (0, j)),
        out_shape=jax.ShapeDtypeStruct((cap, width), rows_in.dtype),
        cost_estimate=pl.CostEstimate(flops=2 * cap * slab * width, transcendentals=0,
            bytes_accessed=2 * (cap * slab + width * slab + 2 * cap * width) + 4 * width),
    )(gated, gathered, rows_in, steer.reshape(1, width), live.astype(jnp.int32).reshape(cap, 1))

def per_device(
    tokens,
    lengths,
    norm_gain,
    w_in,
    short_filter,
    decay_rate,
    residue,
    skip_gain,
    w_out,
    steer_table,
    steer_layer,
    steer_slab,
):
    cap = tokens.shape[2]
    width = tokens.shape[3]
    slab = residue.shape[1]
    groups = lax.axis_size("ctx")
    rows_in = tokens.reshape(cap, width)
    normed = normalize(rows_in, norm_gain)
    position = lax.axis_index("ctx")
    group_lens = lengths.reshape(-1)
    own_len = lax.dynamic_index_in_dim(group_lens, position, 0, keepdims=False)
    live = jnp.arange(cap) < own_len
    own_tail = lax.dynamic_slice_in_dim(normed, own_len - 2, 2, 0)
    tail_normed = from_behind(own_tail, "ctx", 1)

    block = BLOCK if cap % BLOCK == 0 else cap
    toeplitz, lead, close = filter_tables(decay_rate, residue, block)

    lens_f = group_lens.astype(jnp.float32)
    cumlen = jnp.cumsum(lens_f)
    rescale = jnp.exp(decay_rate * (cap - own_len).astype(jnp.float32))

    piece = pack_weights(w_in, w_out)
    gathered = lax.all_gather(piece, "dp", axis=0, tiled=True)
    w_in_all = gathered[:, : 3 * slab]
    rows_ext = jnp.concatenate([tail_normed, normed], axis=0)
    powers = block_powers(decay_rate, cap // block, block)
    starts = (jnp.arange(cap // block) * block).astype(jnp.float32)
    reach = jnp.exp(-decay_rate[None] * starts[:, None, None])
    rows_ext, powers, reach, toeplitz, lead, close = lax.optimization_barrier(
        (rows_ext, powers, reach, toeplitz, lead, close)
    )
    extended = jnp.dot(rows_ext, w_in_all, preferred_element_type=jnp.float32)
    extended = lax.reduce_precision(extended, exponent_bits=8, mantissa_bits=7)
    feat = (
        short_filter[0] * extended[2:]
        + short_filter[1] * extended[1:-1]
        + short_filter[2] * extended[:-2]
    )
    gate = feat[:, :slab]
    drive = jnp.where(live[:, None], feat[:, slab : 2 * slab] * feat[:, 2 * slab :], 0.0)
    states = block_states(drive, powers, close, block)
    ending = states[-1] * rescale
    incoming = jnp.zeros_like(ending)
    for k in range(1, groups):
        got = from_behind(ending, "ctx", k)
        source = position - k
        between = lax.dynamic_index_in_dim(
            cumlen, jnp.maximum(position - 1, 0), 0, keepdims=False
        ) - lax.dynamic_index_in_dim(cumlen, jnp.maximum(source, 0), 0, keepdims=False)
        weight = jnp.where(source >= 0, jnp.exp(-decay_rate * between), 0.0)
        incoming = incoming + weight * got
    local = block_outputs(drive, states, incoming, reach, toeplitz, lead, block)
    filtered = local + skip_gain[None, :] * drive
    gated = jnp.where(live[:, None], gate * filtered, 0.0).astype(jnp.bfloat16)
    rows2 = lax.dynamic_index_in_dim(steer_table, steer_layer[0], 0, keepdims=False)
    shift_vec = rows2[0] - rows2[1]
    columns = jnp.arange(width) // STEER_W
    steer = jnp.where(columns == steer_slab[0], 2.0 * shift_vec, 0.0)
    result = project_out(gated, gathered, rows_in, steer, live)
    return result.reshape(tokens.shape)


def solution(mesh):
    placed = (
        P("dp", "ctx", None, None),
        P("dp", None),
        P(),
        P("dp", None),
        P(),
        P(),
        P(),
        P(),
        P(None, "dp"),
        P(),
        P("dp"),
        P("dp"),
    )
    return jax.shard_map(
        per_device,
        mesh=mesh,
        in_specs=placed,
        out_specs=P("dp", "ctx", None, None),
        check_vma=False,
    )
```

```python
import jax
import jax.numpy as jnp
from jax import lax
from jax.experimental import pallas as pl
from jax.sharding import PartitionSpec as P

STEER_W = 1024
BLOCK = 32


def from_behind(value, axis, steps):
    count = lax.axis_size(axis)
    first, last = (max(0, -steps), min(count, count - steps))
    return lax.ppermute(value, axis, [(source, source + steps) for source in range(first, last)])


def normalize(rows_in, gain):
    values = rows_in.astype(jnp.float32)
    scale = lax.rsqrt(jnp.mean(values * values, axis=1, keepdims=True) + 1e-06)
    return (values * scale * gain[None, :]).astype(jnp.bfloat16)


def filter_tables(decay_rate, residue, block):
    lags = jnp.arange(block)
    lags_float = lags.astype(jnp.float32)
    taps = jnp.sum(residue[None] * jnp.exp(-decay_rate[None] * lags_float[:, None, None]), axis=1)
    diff = lags[:, None] - lags[None, :]
    toeplitz = jnp.where((diff >= 0)[:, :, None], taps[jnp.clip(diff, 0, block - 1)], 0.0)
    toeplitz = jnp.transpose(toeplitz, (1, 0, 2))
    lead = residue[:, None] * jnp.exp(-decay_rate[:, None] * (lags_float + 1.0)[None, :, None])
    close = jnp.exp(-decay_rate[None] * (block - 1 - lags_float)[:, None, None])
    return toeplitz, lead, close


def block_powers(decay_rate, count, block):
    steps = jnp.arange(count)
    gap = (steps[:, None] - steps[None, :]).astype(jnp.float32)
    return jnp.where(
        (gap >= 0)[:, :, None, None],
        jnp.exp(-decay_rate[None, None] * (block * jnp.maximum(gap, 0.0))[:, :, None, None]),
        0.0,
    )


def block_states(drive, powers, close, block):
    cap, width = drive.shape
    pieces = drive.reshape(cap // block, block, width)
    ends = jnp.sum(close[None] * pieces[:, :, None, :], axis=1)
    return jnp.sum(powers * ends[None], axis=1)


def block_outputs(drive, states, incoming, reach, toeplitz, lead, block):
    cap, width = drive.shape
    count = cap // block
    pieces = drive.reshape(count, block, width)
    inside = jnp.sum(toeplitz[None] * pieces[:, :, None, :], axis=1)
    carried = incoming[None] * reach
    before = jnp.concatenate([jnp.zeros_like(states[:1]), states[:-1]], axis=0) + carried
    earlier = jnp.sum(lead[None] * before[:, :, None, :], axis=1)
    return (inside + earlier).reshape(cap, width)


def pack_kernel(wi_ref, wo_ref, o_ref):
    cols = wi_ref.shape[1]
    o_ref[:, :cols] = wi_ref[...]
    o_ref[:, cols:] = wo_ref[...].astype(jnp.float32).T.astype(o_ref.dtype)


def pack_weights(w_in, w_out):
    rows, cols = w_in.shape
    slab = w_out.shape[0]
    step = rows
    return pl.pallas_call(
        pack_kernel,
        grid=(rows // step,),
        in_specs=[
            pl.BlockSpec((step, cols), lambda i: (i, 0)),
            pl.BlockSpec((slab, step), lambda i: (0, i)),
        ],
        out_specs=pl.BlockSpec((step, cols + slab), lambda i: (i, 0)),
        out_shape=jax.ShapeDtypeStruct((rows, cols + slab), w_in.dtype),
    )(w_in, w_out)

def out_kernel(g_ref, w_ref, t_ref, s_ref, m_ref, o_ref):
    acc = lax.dot_general(g_ref[...], w_ref[...], (((1,), (1,)), ((), ())), preferred_element_type=jnp.float32)
    res = t_ref[...].astype(jnp.float32) + acc + s_ref[...]
    o_ref[...] = jnp.where(m_ref[...] > 0, res, 0.0).astype(o_ref.dtype)

def project_out(gated, gathered, rows_in, steer, live, tile=4096):
    cap, slab = gated.shape
    width = rows_in.shape[1]
    tile = tile if width % tile == 0 else width
    column = (gathered.shape[1] - slab) // slab
    return pl.pallas_call(
        out_kernel,
        grid=(width // tile,),
        in_specs=[
            pl.BlockSpec((cap, slab), lambda j: (0, 0)),
            pl.BlockSpec((tile, slab), lambda j: (j, column)),
            pl.BlockSpec((cap, tile), lambda j: (0, j)),
            pl.BlockSpec((1, tile), lambda j: (0, j)),
            pl.BlockSpec((cap, 1), lambda j: (0, 0)),
        ],
        out_specs=pl.BlockSpec((cap, tile), lambda j: (0, j)),
        out_shape=jax.ShapeDtypeStruct((cap, width), rows_in.dtype),
        cost_estimate=pl.CostEstimate(flops=2 * cap * slab * width, transcendentals=0,
            bytes_accessed=2 * (cap * slab + width * slab + 2 * cap * width) + 4 * width),
    )(gated, gathered, rows_in, steer.reshape(1, width), live.astype(jnp.int32).reshape(cap, 1))

def per_device(
    tokens,
    lengths,
    norm_gain,
    w_in,
    short_filter,
    decay_rate,
    residue,
    skip_gain,
    w_out,
    steer_table,
    steer_layer,
    steer_slab,
):
    cap = tokens.shape[2]
    width = tokens.shape[3]
    slab = residue.shape[1]
    groups = lax.axis_size("ctx")
    rows_in = tokens.reshape(cap, width)
    normed = normalize(rows_in, norm_gain)
    position = lax.axis_index("ctx")
    group_lens = lengths.reshape(-1)
    own_len = lax.dynamic_index_in_dim(group_lens, position, 0, keepdims=False)
    live = jnp.arange(cap) < own_len
    own_tail = lax.dynamic_slice_in_dim(normed, own_len - 2, 2, 0)
    tail_normed = from_behind(own_tail, "ctx", 1)

    block = BLOCK if cap % BLOCK == 0 else cap
    toeplitz, lead, close = filter_tables(decay_rate, residue, block)

    lens_f = group_lens.astype(jnp.float32)
    cumlen = jnp.cumsum(lens_f)
    rescale = jnp.exp(decay_rate * (cap - own_len).astype(jnp.float32))

    piece = pack_weights(w_in, w_out)
    gathered = lax.all_gather(piece, "dp", axis=0, tiled=True)
    w_in_all = gathered[:, : 3 * slab]
    rows_ext = jnp.concatenate([tail_normed, normed], axis=0)
    powers = block_powers(decay_rate, cap // block, block)
    starts = (jnp.arange(cap // block) * block).astype(jnp.float32)
    reach = jnp.exp(-decay_rate[None] * starts[:, None, None])
    rows_ext, powers, reach = lax.optimization_barrier((rows_ext, powers, reach))
    extended = jnp.dot(rows_ext, w_in_all, preferred_element_type=jnp.float32)
    extended = lax.reduce_precision(extended, exponent_bits=8, mantissa_bits=7)
    feat = (
        short_filter[0] * extended[2:]
        + short_filter[1] * extended[1:-1]
        + short_filter[2] * extended[:-2]
    )
    gate = feat[:, :slab]
    drive = jnp.where(live[:, None], feat[:, slab : 2 * slab] * feat[:, 2 * slab :], 0.0)
    states = block_states(drive, powers, close, block)
    ending = states[-1] * rescale
    incoming = jnp.zeros_like(ending)
    for k in range(1, groups):
        got = from_behind(ending, "ctx", k)
        source = position - k
        between = lax.dynamic_index_in_dim(
            cumlen, jnp.maximum(position - 1, 0), 0, keepdims=False
        ) - lax.dynamic_index_in_dim(cumlen, jnp.maximum(source, 0), 0, keepdims=False)
        weight = jnp.where(source >= 0, jnp.exp(-decay_rate * between), 0.0)
        incoming = incoming + weight * got
    local = block_outputs(drive, states, incoming, reach, toeplitz, lead, block)
    filtered = local + skip_gain[None, :] * drive
    gated = jnp.where(live[:, None], gate * filtered, 0.0).astype(jnp.bfloat16)
    rows2 = lax.dynamic_index_in_dim(steer_table, steer_layer[0], 0, keepdims=False)
    shift_vec = rows2[0] - rows2[1]
    columns = jnp.arange(width) // STEER_W
    steer = jnp.where(columns == steer_slab[0], 2.0 * shift_vec, 0.0)
    result = project_out(gated, gathered, rows_in, steer, live)
    return result.reshape(tokens.shape)


def solution(mesh):
    placed = (
        P("dp", "ctx", None, None),
        P("dp", None),
        P(),
        P("dp", None),
        P(),
        P(),
        P(),
        P(),
        P(None, "dp"),
        P(),
        P("dp"),
        P("dp"),
    )
    return jax.shard_map(
        per_device,
        mesh=mesh,
        in_specs=placed,
        out_specs=P("dp", "ctx", None, None),
        check_vma=False,
    )
```
